32 devices in a mesh: rows: 8 (over z, x), cols: 4 (over y, core).
Axes of the slice: x: 2, y: 2, z: 4, core: 2. Of those that a mesh axis runs over, the one named last changes fastest.
Arguments:
- vectors: bfloat16 [64, 131072], P('cols', 'rows'), may hold values from -110 to 110
- tile_vals: bfloat16 [1536, 256, 256], P('rows'), may hold values from -0.21875 to 0.21875
- tile_row: int32 [8, 192], P('rows'), may hold values from 0 to 63
- tile_src: int32 [8, 192], P('rows'), may hold values from 0 to 191, each once within a row
- send_list: int32 [64, 16], P('rows'), may hold values from 0 to 63
- ritz_matrix: bfloat16 [64, 64], P(None, 'cols'), may hold values from -0.75 to 0.75
Outputs:
- rotated: bfloat16 [64, 131072], P('cols', 'rows')
- gram_matrix: float32 [64, 64], P('cols')
- projected: float32 [64, 64], P('cols')
The draws below stay inside these ranges and needn't reach their ends.
Inputs may be any that keep to these rules, and one draw needn't show every extreme that they name: Each row of tile_src holds every number once, so that each own or received block is read by exactly one tile.
All inputs are finite; a program needn't handle non-finite values.
Results may differ from the reference program's by a relative error of at most 0.0062.
Values may be sent and summed in bfloat16 or wider, within the bound.
No kernel may reach another device: no remote copies, remote signals or barrier semaphores. Data moves between devices by JAX's collectives and lax.ppermute only.
A program may use at most 128 MiB of HBM per device.

```python
import math
import jax
import jax.numpy as jnp
import numpy as np
from jax import lax

B = 256
K = 64
BR_DEV = 64
SLOT = 16
TILES_DEV = 192
TILES = 1536
NODES = 131072
N_ROWS = 8


def draw_vectors(key, part):
    key_a, key_b, key_c = jax.random.split(key, 3)
    col_scale = jnp.exp(jax.random.uniform(key_a, (K, 1), minval=-1.15, maxval=1.15))
    node_scale = jnp.exp(jax.random.uniform(key_b, (1, NODES), minval=-1.15, maxval=1.15))
    position_scale = jnp.exp(math.log(3.0) * (jnp.arange(NODES, dtype=jnp.float32)[None, :] / NODES - 0.5))
    base_value = jnp.clip(jax.random.normal(key_c, (K, NODES)), -6.0, 6.0)
    return (base_value * col_scale * node_scale * position_scale).astype(jnp.bfloat16)


def place_ends(array, rng, least, largest):
    index_at = [jax.random.randint(jax.random.fold_in(rng, axis), (), 0, length) for axis, length in enumerate(array.shape)]
    longest = array.shape.index(max(array.shape))
    beside = index_at[:longest] + [(index_at[longest] + 1) % array.shape[longest]] + index_at[longest + 1:]
    return array.at[tuple(index_at)].set(least).at[tuple(beside)].set(largest)


def shard_levels(rng, extent, pieces, smallest, high):
    factor_of = 1.0
    for axis_at, blocks in pieces:
        draws = jax.random.uniform(jax.random.fold_in(jax.random.fold_in(rng, 6), axis_at), (blocks,), jnp.float32, smallest / len(pieces), high / len(pieces))
        factor_of = factor_of * jnp.repeat(jnp.exp(draws), extent[axis_at] // blocks).reshape((-1,) + (1,) * (len(extent) - 1 - axis_at))
    return factor_of


def rank_table(amount, slope):
    portions = [(1 << 20) // math.isqrt(standing ** slope) + 1 for standing in range(1, amount + 1)]
    width = 1 + sum(portions) // (1 << 30)
    return np.cumsum(np.array([max(1, weight // width) for weight in portions]))


def ranked_ids(stream_key, shape, amount, skew):
    table = rank_table(amount, skew)
    ticket = jax.random.randint(jax.random.fold_in(stream_key, 1), shape, 0, int(table[amount - 1]))
    rank = jnp.searchsorted(jnp.asarray(table, jnp.int32), ticket, side="right")
    return jax.random.permutation(jax.random.fold_in(stream_key, 2), amount)[rank].astype(jnp.int32)


def scatter_about(key, dims, spread, reach, shards=(), kind=jnp.bfloat16):
    array = spread * jax.random.normal(key, dims, jnp.float32)
    if shards:
        array = array * shard_levels(key, dims, shards, -0.22, 0.18)
    return jnp.clip(array, -reach, reach).astype(kind)


def setup_inputs(seed: int = 0) -> dict:
    seeds = jax.random.split(jax.random.key(seed), 7)
    return {
        "vectors": draw_vectors(jax.random.fold_in(seeds[6], 71), 0),
        "tile_vals": scatter_about(seeds[1], (TILES, B, B), (3 * B) ** -0.5, 0.21875, ((0, 8),)),
        "tile_row": place_ends(ranked_ids(seeds[2], (N_ROWS, TILES_DEV), BR_DEV, 2), jax.random.fold_in(seeds[2], 3), 0, BR_DEV - 1).astype(jnp.int32),
        "tile_src": jax.vmap(lambda own: jax.random.permutation(own, TILES_DEV))(jax.random.split(seeds[3], N_ROWS)).reshape((N_ROWS, TILES_DEV)).astype(jnp.int32),
        "send_list": place_ends(jax.random.randint(seeds[4], (N_ROWS * N_ROWS, SLOT), 0, BR_DEV), jax.random.fold_in(seeds[4], 1), 0, BR_DEV - 1).astype(jnp.int32),
        "ritz_matrix": scatter_about(seeds[5], (K, K), K ** -0.5, 0.75, ((1, 4),)),
    }


def apply_operator(vectors, tile_vals, tile_row, tile_src, send_list):
    columns = vectors.shape[0]
    blocked = vectors.reshape(columns, N_ROWS, BR_DEV, B)
    routes = send_list.reshape(N_ROWS, N_ROWS, SLOT)
    peer_ids = jnp.arange(N_ROWS, dtype=jnp.int32)
    block_ids = jnp.arange(BR_DEV, dtype=jnp.int32)

    def one_device(device):
        own_blocks = lax.dynamic_index_in_dim(blocked, device, 1, keepdims=False)
        wanted = lax.dynamic_index_in_dim(routes, device, 1, keepdims=False)
        incoming = blocked[:, peer_ids[:, None], wanted, :].reshape(columns, N_ROWS * SLOT, B)
        sources = jnp.concatenate([own_blocks, incoming], axis=1)
        tile_block = lax.dynamic_slice_in_dim(tile_vals, device * TILES_DEV, TILES_DEV, 0)
        row_ids = lax.dynamic_index_in_dim(tile_row, device, 0, keepdims=False)
        src_ids = lax.dynamic_index_in_dim(tile_src, device, 0, keepdims=False)
        chosen = jnp.take(sources, src_ids, axis=1).astype(jnp.float32)
        products = jnp.einsum("ktc,trc->ktr", chosen, tile_block.astype(jnp.float32), precision=lax.Precision.HIGHEST)
        onehot = (row_ids[None, :] == block_ids[:, None]).astype(jnp.float32)
        return jnp.einsum("bt,ktr->kbr", onehot, products, precision=lax.Precision.HIGHEST)

    stacked = lax.map(one_device, peer_ids)
    return jnp.transpose(stacked, (1, 0, 2, 3)).reshape(columns, NODES)


def reference(vectors, tile_vals, tile_row, tile_src, send_list, ritz_matrix):
    first_pass = apply_operator(vectors, tile_vals, tile_row, tile_src, send_list).astype(jnp.bfloat16)
    second = apply_operator(first_pass, tile_vals, tile_row, tile_src, send_list)
    filtered = (2.0 * second - vectors.astype(jnp.float32)).astype(jnp.bfloat16)
    operated = apply_operator(filtered, tile_vals, tile_row, tile_src, send_list).astype(jnp.bfloat16)
    gram_matrix = jnp.dot(filtered, filtered.T, preferred_element_type=jnp.float32) / NODES
    projected = jnp.dot(operated, filtered.T, preferred_element_type=jnp.float32) / NODES
    rotated = jnp.dot(ritz_matrix.T, filtered, preferred_element_type=jnp.float32).astype(jnp.bfloat16)
    return (rotated, gram_matrix, projected)
```

```python
import jax
import jax.numpy as jnp
from jax import lax
from jax.sharding import PartitionSpec as P


def tile_products(sources, tile_block, row_ids, src_ids, nblocks):
    chosen = jnp.take(sources, src_ids, axis=1)
    products = jnp.einsum("ktc,trc->ktr", chosen, tile_block, preferred_element_type=jnp.float32)
    onehot = (row_ids[None, :] == jnp.arange(nblocks, dtype=jnp.int32)[:, None]).astype(jnp.float32)
    summed = jnp.einsum("bt,ktr->kbr", onehot, products, precision=lax.Precision.HIGHEST)
    return summed.reshape(summed.shape[0], -1)


def remap_sources(tile_src, nblocks, slot, nrows):
    me = lax.axis_index("rows")
    src = tile_src.reshape(-1)
    peer = (src - nblocks) // slot
    shift = (me - peer) % nrows
    moved = nblocks + shift * slot + (src - nblocks) % slot
    return jnp.where(src < nblocks, src, moved)


def apply_operator(vectors, tile_vals, tile_row, src_ids, send_list):
    columns, length = vectors.shape
    tile_side = tile_vals.shape[1]
    nblocks = length // tile_side
    nrows = send_list.shape[0]
    me = lax.axis_index("rows")
    blocked = vectors.reshape(columns, nblocks, tile_side)
    pieces = []
    for shift in range(nrows):
        dest = (me + shift) % nrows
        wanted = lax.dynamic_index_in_dim(send_list, dest, 0, keepdims=False)
        chunk = jnp.take(blocked, wanted, axis=1)
        if shift:
            pairs = [(i, (i + shift) % nrows) for i in range(nrows)]
            chunk = lax.ppermute(chunk, "rows", pairs)
        pieces.append(chunk)
    row_ids = tile_row.reshape(-1)
    sources = jnp.concatenate([blocked] + pieces, axis=1)
    return tile_products(sources, tile_vals, row_ids, src_ids, nblocks)


def contract_nodes(left_side, right_side):
    return lax.dot_general(
        left_side, right_side, (((1,), (1,)), ((), ())), preferred_element_type=jnp.float32
    )


def tree_sum_rows(value, nrows):
    step = 1
    while step < nrows:
        pairs = [(i, i ^ step) for i in range(nrows)]
        value = value + lax.ppermute(value, "rows", pairs)
        step *= 2
    return value


def gather_cols(piece, ncols):
    half = 2 if ncols % 2 == 0 else 1
    outer = ncols // half
    parts = [piece]
    for shift in range(1, outer):
        pairs = [(i, (i + shift * half) % ncols) for i in range(ncols)]
        parts.append(lax.ppermute(piece, "cols", pairs))
    group = jnp.stack(parts)
    if half == 2:
        pairs = [(i, i ^ 1) for i in range(ncols)]
        other = lax.ppermute(group, "cols", pairs)
        me = lax.axis_index("cols")
        low = me % 2 == 0
        group = jnp.where(low, jnp.stack([group, other], 1), jnp.stack([other, group], 1))
        group = group.reshape((outer * half,) + piece.shape)
    else:
        group = group.reshape((outer,) + piece.shape)
    me = lax.axis_index("cols")
    m = jnp.arange(ncols)
    outer_of = (me // half + m // half) % outer
    absolute = outer_of * half + m % half
    order = jnp.zeros((ncols,), jnp.int32).at[absolute].set(m.astype(jnp.int32))
    group = jnp.take(group, order, axis=0)
    return group.reshape((ncols * piece.shape[0],) + piece.shape[1:])


def body(vectors, tile_vals, tile_row, tile_src, send_list, ritz_matrix):
    tile_side = tile_vals.shape[1]
    nblocks = vectors.shape[1] // tile_side
    nrows = lax.axis_size("rows")
    ncols = lax.axis_size("cols")
    slot = send_list.shape[1]
    src_ids = remap_sources(tile_src, nblocks, slot, nrows)
    first_pass = apply_operator(vectors, tile_vals, tile_row, src_ids, send_list).astype(
        jnp.bfloat16
    )
    second = apply_operator(first_pass, tile_vals, tile_row, src_ids, send_list)
    filtered = (2.0 * second - vectors.astype(jnp.float32)).astype(jnp.bfloat16)
    total_nodes = vectors.shape[1] * nrows
    portion = gather_cols(filtered, ncols)
    operated = apply_operator(filtered, tile_vals, tile_row, src_ids, send_list).astype(
        jnp.bfloat16
    )
    gram_piece = contract_nodes(filtered, portion)
    proj_piece = contract_nodes(operated, portion)
    turned = lax.dot_general(
        ritz_matrix, portion, (((0,), (0,)), ((), ())), preferred_element_type=jnp.float32
    )
    both = tree_sum_rows(jnp.stack([gram_piece, proj_piece]), nrows)
    gram_matrix = both[0] / total_nodes
    projected = both[1] / total_nodes
    rotated = turned.astype(jnp.bfloat16)
    return (rotated, gram_matrix, projected)


def solution(mesh):
    return jax.shard_map(
        body,
        mesh=mesh,
        in_specs=(
            P("cols", "rows"),
            P("rows", None, None),
            P("rows", None),
            P("rows", None),
            P("rows", None),
            P(None, "cols"),
        ),
        out_specs=(P("cols", "rows"), P("cols", None), P("cols", None)),
        check_vma=False,
    )
```

```python
import functools

import jax
import jax.numpy as jnp
from jax import lax
from jax.experimental import pallas as pl
from jax.experimental.pallas import tpu as pltpu
from jax.sharding import PartitionSpec as P

NBUF = 8


def tile_kernel(order_ref, row_ref, src_ref, *refs, first, counts):
    nsrc = len(counts)
    sources = refs[:nsrc]
    tiles_hbm = refs[nsrc]
    out_ref = refs[nsrc + 1]
    buf = refs[nsrc + 2]
    sem = refs[nsrc + 3]
    total = sum(counts)
    out_ref[...] = jnp.zeros(out_ref.shape, out_ref.dtype)

    def copy(j, slot):
        return pltpu.make_async_copy(tiles_hbm.at[order_ref[first + j]], buf.at[slot], sem.at[slot])

    for j in range(min(NBUF, total)):
        copy(j, j).start()
    base = 0
    for k, cnt in enumerate(counts):

        def step(q, carry, k=k, base=base):
            j = base + q
            slot = j % NBUF
            copy(j, slot).wait()
            lhs = sources[k][src_ref[first + j]]
            prod = lax.dot_general(
                lhs, buf[slot], (((1,), (1,)), ((), ())), preferred_element_type=jnp.float32
            )
            r = row_ref[first + j]
            out_ref[r] = out_ref[r] + prod

            @pl.when(j + NBUF < total)
            def _():
                copy(j + NBUF, slot).start()

            return carry

        lax.fori_loop(0, cnt, step, 0)
        base += cnt


def run_tiles(order, rowof, srcof, sources, tile_vals, first, counts, nblocks):
    columns, side = sources[0].shape[1], sources[0].shape[2]
    kernel = functools.partial(tile_kernel, first=first, counts=tuple(counts))
    in_specs = [pl.BlockSpec(memory_space=pltpu.VMEM) for _ in sources]
    in_specs.append(pl.BlockSpec(memory_space=pl.ANY))
    return pl.pallas_call(
        kernel,
        out_shape=jax.ShapeDtypeStruct((nblocks, columns, side), jnp.float32),
        grid_spec=pltpu.PrefetchScalarGridSpec(
            num_scalar_prefetch=3,
            grid=(1,),
            in_specs=in_specs,
            out_specs=pl.BlockSpec(memory_space=pltpu.VMEM),
            scratch_shapes=[
                pltpu.VMEM((NBUF,) + tile_vals.shape[1:], tile_vals.dtype),
                pltpu.SemaphoreType.DMA((NBUF,)),
            ],
        ),
    )(order, rowof, srcof, *sources, tile_vals)


def plan_slots(tile_row, tile_src, send_list):
    nrows, slot = send_list.shape
    ntiles = tile_src.shape[-1]
    nblocks = ntiles - nrows * slot
    me = lax.axis_index("rows")
    src = tile_src.reshape(-1)
    peer = (src - nblocks) // slot
    shift = (me - peer) % nrows
    moved = nblocks + shift * slot + (src - nblocks) % slot
    slots = jnp.where(src < nblocks, src, moved)
    order = jnp.zeros((ntiles,), jnp.int32).at[slots].set(jnp.arange(ntiles, dtype=jnp.int32))
    rowof = jnp.take(tile_row.reshape(-1), order)
    j = jnp.arange(ntiles, dtype=jnp.int32)
    mine = lax.dynamic_index_in_dim(send_list, me, 0, keepdims=False)
    q = (j - nblocks) % slot
    srcof = jnp.where(j < nblocks, j, jnp.where(j < nblocks + slot, jnp.take(mine, q), q))
    return order, rowof, srcof.astype(jnp.int32)


def apply_operator(blocked, tile_vals, plan, send_list):
    order, rowof, srcof = plan
    nblocks = blocked.shape[0]
    nrows, slot = send_list.shape
    me = lax.axis_index("rows")
    pieces = []
    for shift in range(1, nrows):
        dest = (me + shift) % nrows
        wanted = lax.dynamic_index_in_dim(send_list, dest, 0, keepdims=False)
        chunk = jnp.take(blocked, wanted, axis=0)
        pairs = [(i, (i + shift) % nrows) for i in range(nrows)]
        pieces.append(lax.ppermute(chunk, "rows", pairs))
    own = run_tiles(order, rowof, srcof, [blocked], tile_vals, 0, [nblocks + slot], nblocks)
    received = run_tiles(
        order, rowof, srcof, pieces, tile_vals, nblocks + slot, [slot] * (nrows - 1), nblocks
    )
    return own + received


def tree_sum_rows(value, nrows):
    step = 1
    while step < nrows:
        pairs = [(i, i ^ step) for i in range(nrows)]
        value = value + lax.ppermute(value, "rows", pairs)
        step *= 2
    return value


def gather_cols(piece, ncols):
    half = 2 if ncols % 2 == 0 else 1
    outer = ncols // half
    me = lax.axis_index("cols")
    parts, owners = [piece], [me]
    for shift in range(1, outer):
        pairs = [(i, (i + shift * half) % ncols) for i in range(ncols)]
        parts.append(lax.ppermute(piece, "cols", pairs))
        owners.append((me - shift * half) % ncols)
    if half == 2:
        pairs = [(i, i ^ 1) for i in range(ncols)]
        count = len(parts)
        for n in range(count):
            parts.append(lax.ppermute(parts[n], "cols", pairs))
            owners.append(owners[n] ^ 1)
    return parts, owners


def body(vectors, tile_vals, tile_row, tile_src, send_list, ritz_matrix):
    columns, length = vectors.shape
    side = tile_vals.shape[1]
    nblocks = length // side
    nrows = lax.axis_size("rows")
    ncols = lax.axis_size("cols")
    plan = plan_slots(tile_row, tile_src, send_list)
    start = vectors.reshape(columns, nblocks, side).transpose(1, 0, 2)
    first_pass = apply_operator(start, tile_vals, plan, send_list).astype(jnp.bfloat16)
    second = apply_operator(first_pass, tile_vals, plan, send_list)
    filtered = (2.0 * second - start.astype(jnp.float32)).astype(jnp.bfloat16)
    total_nodes = length * nrows
    parts, owners = gather_cols(filtered, ncols)
    operated = apply_operator(filtered, tile_vals, plan, send_list).astype(jnp.bfloat16)
    contract = (((0, 2), (0, 2)), ((), ()))
    gram_cols = [lax.dot_general(filtered, p, contract, preferred_element_type=jnp.float32) for p in parts]
    proj_cols = [lax.dot_general(operated, p, contract, preferred_element_type=jnp.float32) for p in parts]
    owner_ids = jnp.stack(owners).astype(jnp.int32)
    place = jnp.zeros((ncols,), jnp.int32).at[owner_ids].set(jnp.arange(ncols, dtype=jnp.int32))
    gram_rel = jnp.stack(gram_cols)
    proj_rel = jnp.stack(proj_cols)
    both = jnp.stack([jnp.take(gram_rel, place, axis=0), jnp.take(proj_rel, place, axis=0)])
    both = both.transpose(0, 2, 1, 3).reshape(2, columns, ncols * columns)
    both = tree_sum_rows(both, nrows)
    gram_matrix = both[0] / total_nodes
    projected = both[1] / total_nodes
    ritz_rows = ritz_matrix.reshape(ncols, columns, ritz_matrix.shape[1])
    turned = None
    for p, owner in zip(parts, owners):
        weights = lax.dynamic_index_in_dim(ritz_rows, owner, 0, keepdims=False)
        term = jnp.einsum("ij,bic->jbc", weights, p, preferred_element_type=jnp.float32)
        turned = term if turned is None else turned + term
    rotated = turned.astype(jnp.bfloat16).reshape(ritz_matrix.shape[1], length)
    return (rotated, gram_matrix, projected)


def solution(mesh):
    return jax.shard_map(
        body,
        mesh=mesh,
        in_specs=(
            P("cols", "rows"),
            P("rows", None, None),
            P("rows", None),
            P("rows", None),
            P("rows", None),
            P(None, "cols"),
        ),
        out_specs=(P("cols", "rows"), P("cols", None), P("cols", None)),
        check_vma=False,
    )
```

```python
import jax
import jax.numpy as jnp
from jax import lax
from jax.sharding import PartitionSpec as P

def plan_slots(tile_row, tile_src, send_list):
    nrows, slot = send_list.shape
    ntiles = tile_src.shape[-1]
    nblocks = ntiles - nrows * slot
    me = lax.axis_index("rows")
    src = tile_src.reshape(-1)
    peer = (src - nblocks) // slot
    shift = (me - peer) % nrows
    moved = nblocks + shift * slot + (src - nblocks) % slot
    slots = jnp.where(src < nblocks, src, moved)
    order = jnp.zeros((ntiles,), jnp.int32).at[slots].set(jnp.arange(ntiles, dtype=jnp.int32))
    rowof = jnp.take(tile_row.reshape(-1), order)
    j = jnp.arange(ntiles, dtype=jnp.int32)
    mine = lax.dynamic_index_in_dim(send_list, me, 0, keepdims=False)
    q = (j - nblocks) % slot
    srcof = jnp.where(j < nblocks, j, jnp.where(j < nblocks + slot, jnp.take(mine, q), q))
    return order, rowof, srcof.astype(jnp.int32)


def exchange(blocked, send_list):
    nrows = send_list.shape[0]
    me = lax.axis_index("rows")
    pieces = []
    for shift in range(1, nrows):
        dest = (me + shift) % nrows
        wanted = lax.dynamic_index_in_dim(send_list, dest, 0, keepdims=False)
        chunk = jnp.take(blocked, wanted, axis=0)
        pairs = [(i, (i + shift) % nrows) for i in range(nrows)]
        pieces.append(lax.ppermute(chunk, "rows", pairs))
    mine = lax.dynamic_index_in_dim(send_list, me, 0, keepdims=False)
    return jnp.take(blocked, mine, axis=0), pieces


def row_sum(onehot, products):
    return jnp.einsum("bj,jkr->bkr", onehot, products, precision=lax.Precision.HIGHEST)


def products_of(sources, tiles):
    return jnp.einsum("jkc,jrc->jkr", sources, tiles, preferred_element_type=jnp.float32)


def first_apply(blocked, tile_vals, plan, send_list):
    order, rowof, _ = plan
    nblocks = blocked.shape[0]
    own_self, pieces = exchange(blocked, send_list)
    sources = jnp.concatenate([blocked, own_self] + pieces, axis=0)
    slot_of_tile = jnp.zeros_like(order).at[order].set(jnp.arange(order.shape[0], dtype=order.dtype))
    chosen = jnp.take(sources, slot_of_tile, axis=0)
    products = products_of(chosen, tile_vals)
    rows = jnp.take(rowof, slot_of_tile)
    onehot = (rows[None, :] == jnp.arange(nblocks, dtype=jnp.int32)[:, None]).astype(jnp.float32)
    return row_sum(onehot, products)


def sorted_apply(blocked, tiles_sorted, onehot, send_list):
    nblocks = blocked.shape[0]
    slot = send_list.shape[1]
    own_self, pieces = exchange(blocked, send_list)
    split = nblocks + slot
    own = products_of(jnp.concatenate([blocked, own_self], axis=0), tiles_sorted[:split])
    out = row_sum(onehot[:, :split], own)
    received = products_of(jnp.concatenate(pieces, axis=0), tiles_sorted[split:])
    return out + row_sum(onehot[:, split:], received)


def tree_sum_rows(value, nrows):
    step = 1
    while step < nrows:
        pairs = [(i, i ^ step) for i in range(nrows)]
        value = value + lax.ppermute(value, "rows", pairs)
        step *= 2
    return value


def gather_cols(piece, ncols):
    half = 2 if ncols % 2 == 0 else 1
    outer = ncols // half
    me = lax.axis_index("cols")
    parts, owners = [piece], [me]
    for shift in range(1, outer):
        pairs = [(i, (i + shift * half) % ncols) for i in range(ncols)]
        parts.append(lax.ppermute(piece, "cols", pairs))
        owners.append((me - shift * half) % ncols)
    if half == 2:
        pairs = [(i, i ^ 1) for i in range(ncols)]
        count = len(parts)
        for n in range(count):
            parts.append(lax.ppermute(parts[n], "cols", pairs))
            owners.append(owners[n] ^ 1)
    return parts, owners


def body(vectors, tile_vals, tile_row, tile_src, send_list, ritz_matrix):
    columns, length = vectors.shape
    side = tile_vals.shape[1]
    nblocks = length // side
    nrows = lax.axis_size("rows")
    ncols = lax.axis_size("cols")
    plan = plan_slots(tile_row, tile_src, send_list)
    start = vectors.reshape(columns, nblocks, side).transpose(1, 0, 2)
    first_pass = first_apply(start, tile_vals, plan, send_list).astype(jnp.bfloat16)
    order, rowof, _ = plan
    tiles_sorted = jnp.take(tile_vals, order, axis=0)
    onehot = (rowof[None, :] == jnp.arange(nblocks, dtype=jnp.int32)[:, None]).astype(jnp.float32)
    second = sorted_apply(first_pass, tiles_sorted, onehot, send_list)
    filtered = (2.0 * second - start.astype(jnp.float32)).astype(jnp.bfloat16)
    total_nodes = length * nrows
    parts, owners = gather_cols(filtered, ncols)
    operated = sorted_apply(filtered, tiles_sorted, onehot, send_list).astype(jnp.bfloat16)
    contract = (((0, 2), (0, 2)), ((), ()))
    gram_cols = [lax.dot_general(filtered, p, contract, preferred_element_type=jnp.float32) for p in parts]
    proj_cols = [lax.dot_general(operated, p, contract, preferred_element_type=jnp.float32) for p in parts]
    owner_ids = jnp.stack(owners).astype(jnp.int32)
    place = jnp.zeros((ncols,), jnp.int32).at[owner_ids].set(jnp.arange(ncols, dtype=jnp.int32))
    gram_rel = jnp.stack(gram_cols)
    proj_rel = jnp.stack(proj_cols)
    both = jnp.stack([jnp.take(gram_rel, place, axis=0), jnp.take(proj_rel, place, axis=0)])
    both = both.transpose(0, 2, 1, 3).reshape(2, columns, ncols * columns)
    both = tree_sum_rows(both, nrows)
    gram_matrix = both[0] / total_nodes
    projected = both[1] / total_nodes
    ritz_rows = ritz_matrix.reshape(ncols, columns, ritz_matrix.shape[1])
    turned = None
    for p, owner in zip(parts, owners):
        weights = lax.dynamic_index_in_dim(ritz_rows, owner, 0, keepdims=False)
        term = jnp.einsum("ij,bic->jbc", weights, p, preferred_element_type=jnp.float32)
        turned = term if turned is None else turned + term
    rotated = turned.astype(jnp.bfloat16).reshape(ritz_matrix.shape[1], length)
    return (rotated, gram_matrix, projected)


def solution(mesh):
    return jax.shard_map(
        body,
        mesh=mesh,
        in_specs=(
            P("cols", "rows"),
            P("rows", None, None),
            P("rows", None),
            P("rows", None),
            P("rows", None),
            P(None, "cols"),
        ),
        out_specs=(P("cols", "rows"), P("cols", None), P("cols", None)),
        check_vma=False,
    )
```

```python
import jax
import jax.numpy as jnp
from jax import lax
from jax.sharding import PartitionSpec as P


def plan_slots(tile_row, tile_src, send_list):
    nrows, slot = send_list.shape
    ntiles = tile_src.shape[-1]
    nblocks = ntiles - nrows * slot
    me = lax.axis_index("rows")
    src = tile_src.reshape(-1)
    peer = (src - nblocks) // slot
    shift = (me - peer) % nrows
    moved = nblocks + shift * slot + (src - nblocks) % slot
    slots = jnp.where(src < nblocks, src, moved)
    order = jnp.zeros((ntiles,), jnp.int32).at[slots].set(jnp.arange(ntiles, dtype=jnp.int32))
    rowof = jnp.take(tile_row.reshape(-1), order, mode="clip")
    j = jnp.arange(ntiles, dtype=jnp.int32)
    mine = lax.dynamic_index_in_dim(send_list, me, 0, keepdims=False)
    q = (j - nblocks) % slot
    srcof = jnp.where(j < nblocks, j, jnp.where(j < nblocks + slot, jnp.take(mine, q, mode="clip"), q))
    return order, rowof, srcof.astype(jnp.int32)


def exchange(blocked, send_list):
    nrows = send_list.shape[0]
    me = lax.axis_index("rows")
    pieces = []
    for shift in range(1, nrows):
        dest = (me + shift) % nrows
        wanted = lax.dynamic_index_in_dim(send_list, dest, 0, keepdims=False)
        chunk = jnp.take(blocked, wanted, axis=0, mode="clip")
        pairs = [(i, (i + shift) % nrows) for i in range(nrows)]
        pieces.append(lax.ppermute(chunk, "rows", pairs))
    mine = lax.dynamic_index_in_dim(send_list, me, 0, keepdims=False)
    return jnp.take(blocked, mine, axis=0, mode="clip"), pieces


def row_sum(onehot, products):
    return jnp.einsum("bj,jkr->bkr", onehot, products, precision=lax.Precision.HIGHEST)


def products_of(sources, tiles):
    return jnp.einsum("jkc,jrc->jkr", sources, tiles, preferred_element_type=jnp.float32)


def first_apply(blocked, tile_vals, plan, send_list):
    order, rowof, _ = plan
    nblocks = blocked.shape[0]
    own_self, pieces = exchange(blocked, send_list)
    sources = jnp.concatenate([blocked, own_self] + pieces, axis=0)
    slot_of_tile = jnp.zeros_like(order).at[order].set(jnp.arange(order.shape[0], dtype=order.dtype))
    chosen = jnp.take(sources, slot_of_tile, axis=0, mode="clip")
    products = products_of(chosen, tile_vals)
    rows = jnp.take(rowof, slot_of_tile, mode="clip")
    onehot = (rows[None, :] == jnp.arange(nblocks, dtype=jnp.int32)[:, None]).astype(jnp.float32)
    return row_sum(onehot, products)


def sorted_apply(blocked, tiles_sorted, onehot, send_list):
    nblocks = blocked.shape[0]
    slot = send_list.shape[1]
    own_self, pieces = exchange(blocked, send_list)
    split = nblocks + slot
    own = products_of(jnp.concatenate([blocked, own_self], axis=0), tiles_sorted[:split])
    out = row_sum(onehot[:, :split], own)
    received = products_of(jnp.concatenate(pieces, axis=0), tiles_sorted[split:])
    return out + row_sum(onehot[:, split:], received)


def tree_sum_rows(value, nrows):
    step = 1
    while step < nrows:
        pairs = [(i, i ^ step) for i in range(nrows)]
        value = value + lax.ppermute(value, "rows", pairs)
        step *= 2
    return value


def gather_cols(piece, ncols):
    half = 2 if ncols % 2 == 0 else 1
    outer = ncols // half
    me = lax.axis_index("cols")
    parts, owners = [piece], [me]
    for shift in range(1, outer):
        pairs = [(i, (i + shift * half) % ncols) for i in range(ncols)]
        parts.append(lax.ppermute(piece, "cols", pairs))
        owners.append((me - shift * half) % ncols)
    if half == 2:
        pairs = [(i, i ^ 1) for i in range(ncols)]
        count = len(parts)
        for n in range(count):
            parts.append(lax.ppermute(parts[n], "cols", pairs))
            owners.append(owners[n] ^ 1)
    return parts, owners


def body(vectors, tile_vals, tile_row, tile_src, send_list, ritz_matrix):
    columns, length = vectors.shape
    side = tile_vals.shape[1]
    nblocks = length // side
    nrows = lax.axis_size("rows")
    ncols = lax.axis_size("cols")
    plan = plan_slots(tile_row, tile_src, send_list)
    start = vectors.reshape(columns, nblocks, side).transpose(1, 0, 2)
    first_pass = first_apply(start, tile_vals, plan, send_list).astype(jnp.bfloat16)
    order, rowof, _ = plan
    tiles_sorted = jnp.take(tile_vals, order, axis=0, mode="clip")
    onehot = (rowof[None, :] == jnp.arange(nblocks, dtype=jnp.int32)[:, None]).astype(jnp.float32)
    second = sorted_apply(first_pass, tiles_sorted, onehot, send_list)
    filtered = (2.0 * second - start.astype(jnp.float32)).astype(jnp.bfloat16)
    total_nodes = length * nrows
    parts, owners = gather_cols(filtered, ncols)
    operated = sorted_apply(filtered, tiles_sorted, onehot, send_list).astype(jnp.bfloat16)
    contract = (((0, 2), (0, 2)), ((), ()))
    gram_cols = [lax.dot_general(filtered, p, contract, preferred_element_type=jnp.float32) for p in parts]
    proj_cols = [lax.dot_general(operated, p, contract, preferred_element_type=jnp.float32) for p in parts]
    owner_ids = jnp.stack(owners).astype(jnp.int32)
    place = jnp.zeros((ncols,), jnp.int32).at[owner_ids].set(jnp.arange(ncols, dtype=jnp.int32))
    gram_rel = jnp.stack(gram_cols)
    proj_rel = jnp.stack(proj_cols)
    both = jnp.stack([jnp.take(gram_rel, place, axis=0, mode="clip"), jnp.take(proj_rel, place, axis=0, mode="clip")])
    both = both.transpose(0, 2, 1, 3).reshape(2, columns, ncols * columns)
    both = tree_sum_rows(both, nrows)
    gram_matrix = both[0] / total_nodes
    projected = both[1] / total_nodes
    ritz_rows = ritz_matrix.reshape(ncols, columns, ritz_matrix.shape[1])
    turned = None
    for p, owner in zip(parts, owners):
        weights = lax.dynamic_index_in_dim(ritz_rows, owner, 0, keepdims=False)
        term = jnp.einsum("ij,bic->jbc", weights, p, preferred_element_type=jnp.float32)
        turned = term if turned is None else turned + term
    rotated = turned.astype(jnp.bfloat16).reshape(ritz_matrix.shape[1], length)
    return (rotated, gram_matrix, projected)


def solution(mesh):
    return jax.shard_map(
        body,
        mesh=mesh,
        in_specs=(
            P("cols", "rows"),
            P("rows", None, None),
            P("rows", None),
            P("rows", None),
            P("rows", None),
            P(None, "cols"),
        ),
        out_specs=(P("cols", "rows"), P("cols", None), P("cols", None)),
        check_vma=False,
    )
```

```python
import jax
import jax.numpy as jnp
from jax import lax
from jax.sharding import PartitionSpec as P


def plan_slots(tile_row, tile_src, send_list):
    nrows, slot = send_list.shape
    ntiles = tile_src.shape[-1]
    nblocks = ntiles - nrows * slot
    me = lax.axis_index("rows")
    src = tile_src.reshape(-1)
    peer = (src - nblocks) // slot
    shift = (me - peer) % nrows
    moved = nblocks + shift * slot + (src - nblocks) % slot
    slots = jnp.where(src < nblocks, src, moved)
    order = jnp.zeros((ntiles,), jnp.int32).at[slots].set(jnp.arange(ntiles, dtype=jnp.int32))
    rowof = jnp.take(tile_row.reshape(-1), order, mode="clip")
    j = jnp.arange(ntiles, dtype=jnp.int32)
    mine = lax.dynamic_index_in_dim(send_list, me, 0, keepdims=False)
    q = (j - nblocks) % slot
    srcof = jnp.where(j < nblocks, j, jnp.where(j < nblocks + slot, jnp.take(mine, q, mode="clip"), q))
    return order, rowof, srcof.astype(jnp.int32)


def exchange(blocked, send_list):
    nrows = send_list.shape[0]
    me = lax.axis_index("rows")
    pieces = []
    for shift in range(1, nrows):
        dest = (me + shift) % nrows
        wanted = lax.dynamic_index_in_dim(send_list, dest, 0, keepdims=False)
        chunk = jnp.take(blocked, wanted, axis=0, mode="clip")
        pairs = [(i, (i + shift) % nrows) for i in range(nrows)]
        pieces.append(lax.ppermute(chunk, "rows", pairs))
    mine = lax.dynamic_index_in_dim(send_list, me, 0, keepdims=False)
    return jnp.take(blocked, mine, axis=0, mode="clip"), pieces


def row_sum(onehot, products):
    return jnp.einsum("bj,jkr->bkr", onehot, products, precision=lax.Precision.HIGHEST)


def products_of(sources, tiles):
    return jnp.einsum("jkc,jrc->jkr", sources, tiles, preferred_element_type=jnp.float32)


def first_apply(blocked, tile_vals, plan, send_list):
    order, rowof, _ = plan
    nblocks = blocked.shape[0]
    own_self, pieces = exchange(blocked, send_list)
    sources = jnp.concatenate([blocked, own_self] + pieces, axis=0)
    slot_of_tile = jnp.zeros_like(order).at[order].set(jnp.arange(order.shape[0], dtype=order.dtype))
    chosen = jnp.take(sources, slot_of_tile, axis=0, mode="clip")
    products = products_of(chosen, tile_vals)
    rows = jnp.take(rowof, slot_of_tile, mode="clip")
    onehot = (rows[None, :] == jnp.arange(nblocks, dtype=jnp.int32)[:, None]).astype(jnp.float32)
    return row_sum(onehot, products)


def sorted_apply(blocked, tiles_sorted, onehot, send_list):
    nblocks = blocked.shape[0]
    slot = send_list.shape[1]
    own_self, pieces = exchange(blocked, send_list)
    split = nblocks + slot
    own = products_of(jnp.concatenate([blocked, own_self], axis=0), tiles_sorted[:split])
    out = row_sum(onehot[:, :split], own)
    received = products_of(jnp.concatenate(pieces, axis=0), tiles_sorted[split:])
    return out + row_sum(onehot[:, split:], received)


def tree_sum_rows(value, nrows):
    step = 1
    while step < nrows:
        pairs = [(i, i ^ step) for i in range(nrows)]
        value = value + lax.ppermute(value, "rows", pairs)
        step *= 2
    return value


def gather_cols(piece, ncols):
    half = 2 if ncols % 2 == 0 else 1
    outer = ncols // half
    me = lax.axis_index("cols")
    parts, owners = [piece], [me]
    for shift in range(1, outer):
        pairs = [(i, (i + shift * half) % ncols) for i in range(ncols)]
        parts.append(lax.ppermute(piece, "cols", pairs))
        owners.append((me - shift * half) % ncols)
    if half == 2:
        pairs = [(i, i ^ 1) for i in range(ncols)]
        count = len(parts)
        for n in range(count):
            parts.append(lax.ppermute(parts[n], "cols", pairs))
            owners.append(owners[n] ^ 1)
    return parts, owners


def body(vectors, tile_vals, tile_row, tile_src, send_list, ritz_matrix):
    columns, length = vectors.shape
    side = tile_vals.shape[1]
    nblocks = length // side
    nrows = lax.axis_size("rows")
    ncols = lax.axis_size("cols")
    plan = plan_slots(tile_row, tile_src, send_list)
    start = vectors.reshape(columns, nblocks, side).transpose(1, 0, 2)
    first_pass = first_apply(start, tile_vals, plan, send_list).astype(jnp.bfloat16)
    order, rowof, _ = plan
    tiles_sorted = jnp.take(tile_vals, order, axis=0, mode="clip")
    onehot = (rowof[None, :] == jnp.arange(nblocks, dtype=jnp.int32)[:, None]).astype(jnp.float32)
    second = sorted_apply(first_pass, tiles_sorted, onehot, send_list)
    filtered = (2.0 * second - start.astype(jnp.float32)).astype(jnp.bfloat16)
    total_nodes = length * nrows
    parts, owners = gather_cols(filtered, ncols)
    operated = sorted_apply(filtered, tiles_sorted, onehot, send_list).astype(jnp.bfloat16)
    contract = (((0, 2), (0, 2)), ((), ()))
    portion = jnp.concatenate(parts, axis=1)
    owner_ids = jnp.stack(owners).astype(jnp.int32)
    place = jnp.zeros((ncols,), jnp.int32).at[owner_ids].set(jnp.arange(ncols, dtype=jnp.int32))
    ritz_rows = ritz_matrix.reshape(ncols, columns, ritz_matrix.shape[1])
    weights = jnp.take(ritz_rows, owner_ids, axis=0, mode="clip").reshape(ritz_matrix.shape)
    turned = jnp.einsum("ij,bic->jbc", weights, portion, preferred_element_type=jnp.float32)
    rotated = turned.astype(jnp.bfloat16).reshape(ritz_matrix.shape[1], length)
    gram_rel = lax.dot_general(filtered, portion, contract, preferred_element_type=jnp.float32)
    proj_rel = lax.dot_general(operated, portion, contract, preferred_element_type=jnp.float32)
    both = jnp.stack([gram_rel, proj_rel]).reshape(2, columns, ncols, columns)
    both = jnp.take(both, place, axis=2, mode="clip").reshape(2, columns, ncols * columns)
    both = tree_sum_rows(both, nrows)
    gram_matrix = both[0] / total_nodes
    projected = both[1] / total_nodes
    return (rotated, gram_matrix, projected)


def solution(mesh):
    return jax.shard_map(
        body,
        mesh=mesh,
        in_specs=(
            P("cols", "rows"),
            P("rows", None, None),
            P("rows", None),
            P("rows", None),
            P("rows", None),
            P(None, "cols"),
        ),
        out_specs=(P("cols", "rows"), P("cols", None), P("cols", None)),
        check_vma=False,
    )
```

```python
import jax
import jax.numpy as jnp
from jax import lax
from jax.sharding import PartitionSpec as P


def plan_slots(tile_row, tile_src, send_list):
    nrows, slot = send_list.shape
    ntiles = tile_src.shape[-1]
    nblocks = ntiles - nrows * slot
    me = lax.axis_index("rows")
    src = tile_src.reshape(-1)
    peer = (src - nblocks) // slot
    shift = (me - peer) % nrows
    moved = nblocks + shift * slot + (src - nblocks) % slot
    slots = jnp.where(src < nblocks, src, moved)
    hit = slots[None, :] == jnp.arange(ntiles, dtype=jnp.int32)[:, None]
    tiles = jnp.arange(ntiles, dtype=jnp.int32)[None, :]
    order = jnp.sum(jnp.where(hit, tiles, 0), axis=1)
    rowof = jnp.sum(jnp.where(hit, tile_row.reshape(1, -1), 0), axis=1)
    return order, rowof, slots


def exchange(blocked, send_list):
    nrows, slot = send_list.shape
    me = lax.axis_index("rows")
    dests = (me + jnp.arange(nrows, dtype=jnp.int32)) % nrows
    wanted = jnp.take(send_list, dests, axis=0, mode="clip").reshape(-1)
    outgoing = jnp.take(blocked, wanted, axis=0, mode="clip")
    pieces = []
    for shift in range(1, nrows):
        chunk = outgoing[shift * slot:(shift + 1) * slot]
        pairs = [(i, (i + shift) % nrows) for i in range(nrows)]
        pieces.append(lax.ppermute(chunk, "rows", pairs))
    return outgoing[:slot], pieces


def row_sum(onehot, products):
    return jnp.einsum("bj,jkr->bkr", onehot, products, precision=lax.Precision.HIGHEST)


def products_of(sources, tiles):
    return jnp.einsum("jkc,jrc->jkr", sources, tiles, preferred_element_type=jnp.float32)


def first_apply(blocked, tile_vals, tile_row, plan, send_list):
    order, rowof, slot_of_tile = plan
    nblocks = blocked.shape[0]
    own_self, pieces = exchange(blocked, send_list)
    sources = jnp.concatenate([blocked, own_self] + pieces, axis=0)
    chosen = jnp.take(sources, slot_of_tile, axis=0, mode="clip")
    products = products_of(chosen, tile_vals)
    onehot = (tile_row.reshape(1, -1) == jnp.arange(nblocks, dtype=jnp.int32)[:, None]).astype(jnp.float32)
    return row_sum(onehot, products)


def sorted_apply(blocked, tiles_sorted, onehot, send_list):
    nblocks = blocked.shape[0]
    slot = send_list.shape[1]
    own_self, pieces = exchange(blocked, send_list)
    split = nblocks + slot
    own = products_of(jnp.concatenate([blocked, own_self], axis=0), tiles_sorted[:split])
    out = row_sum(onehot[:, :split], own)
    received = products_of(jnp.concatenate(pieces, axis=0), tiles_sorted[split:])
    return out + row_sum(onehot[:, split:], received)


def tree_sum_rows(value, nrows):
    step = 1
    while step < nrows:
        pairs = [(i, i ^ step) for i in range(nrows)]
        value = value + lax.ppermute(value, "rows", pairs)
        step *= 2
    return value


def gather_cols(piece, ncols):
    half = 2 if ncols % 2 == 0 else 1
    outer = ncols // half
    me = lax.axis_index("cols")
    parts, owners = [piece], [me]
    for shift in range(1, outer):
        pairs = [(i, (i + shift * half) % ncols) for i in range(ncols)]
        parts.append(lax.ppermute(piece, "cols", pairs))
        owners.append((me - shift * half) % ncols)
    if half == 2:
        pairs = [(i, i ^ 1) for i in range(ncols)]
        count = len(parts)
        for n in range(count):
            parts.append(lax.ppermute(parts[n], "cols", pairs))
            owners.append(owners[n] ^ 1)
    return parts, owners


def body(vectors, tile_vals, tile_row, tile_src, send_list, ritz_matrix):
    columns, length = vectors.shape
    side = tile_vals.shape[1]
    nblocks = length // side
    nrows = lax.axis_size("rows")
    ncols = lax.axis_size("cols")
    plan = plan_slots(tile_row, tile_src, send_list)
    start = vectors.reshape(columns, nblocks, side).transpose(1, 0, 2)
    first_pass = first_apply(start, tile_vals, tile_row, plan, send_list).astype(jnp.bfloat16)
    order, rowof, _ = plan
    tiles_sorted = jnp.take(tile_vals, order, axis=0, mode="clip")
    onehot = (rowof[None, :] == jnp.arange(nblocks, dtype=jnp.int32)[:, None]).astype(jnp.float32)
    second = sorted_apply(first_pass, tiles_sorted, onehot, send_list)
    filtered = (2.0 * second - start.astype(jnp.float32)).astype(jnp.bfloat16)
    total_nodes = length * nrows
    parts, owners = gather_cols(filtered, ncols)
    operated = sorted_apply(filtered, tiles_sorted, onehot, send_list).astype(jnp.bfloat16)
    contract = (((0, 2), (0, 2)), ((), ()))
    portion = jnp.concatenate(parts, axis=1)
    owner_ids = jnp.stack(owners).astype(jnp.int32)
    place = jnp.zeros((ncols,), jnp.int32).at[owner_ids].set(jnp.arange(ncols, dtype=jnp.int32))
    ritz_rows = ritz_matrix.reshape(ncols, columns, ritz_matrix.shape[1])
    weights = jnp.take(ritz_rows, owner_ids, axis=0, mode="clip").reshape(ritz_matrix.shape)
    turned = jnp.einsum("ij,bic->jbc", weights, portion, preferred_element_type=jnp.float32)
    rotated = turned.astype(jnp.bfloat16).reshape(ritz_matrix.shape[1], length)
    gram_rel = lax.dot_general(filtered, portion, contract, preferred_element_type=jnp.float32)
    proj_rel = lax.dot_general(operated, portion, contract, preferred_element_type=jnp.float32)
    both = jnp.stack([gram_rel, proj_rel]).reshape(2, columns, ncols, columns)
    both = jnp.take(both, place, axis=2, mode="clip").reshape(2, columns, ncols * columns)
    both = tree_sum_rows(both, nrows)
    gram_matrix = both[0] / total_nodes
    projected = both[1] / total_nodes
    return (rotated, gram_matrix, projected)


def solution(mesh):
    return jax.shard_map(
        body,
        mesh=mesh,
        in_specs=(
            P("cols", "rows"),
            P("rows", None, None),
            P("rows", None),
            P("rows", None),
            P("rows", None),
            P(None, "cols"),
        ),
        out_specs=(P("cols", "rows"), P("cols", None), P("cols", None)),
        check_vma=False,
    )
```

```python
import jax
import jax.numpy as jnp
from jax import lax
from jax.sharding import PartitionSpec as P


def plan_slots(tile_row, tile_src, send_list):
    nrows, slot = send_list.shape
    ntiles = tile_src.shape[-1]
    nblocks = ntiles - nrows * slot
    me = lax.axis_index("rows")
    src = tile_src.reshape(-1)
    peer = (src - nblocks) // slot
    shift = (me - peer) % nrows
    moved = nblocks + shift * slot + (src - nblocks) % slot
    slots = jnp.where(src < nblocks, src, moved)
    hit = slots[None, :] == jnp.arange(ntiles, dtype=jnp.int32)[:, None]
    tiles = jnp.arange(ntiles, dtype=jnp.int32)[None, :]
    order = jnp.sum(jnp.where(hit, tiles, 0), axis=1)
    rowof = jnp.sum(jnp.where(hit, tile_row.reshape(1, -1), 0), axis=1)
    return order, rowof, slots


def exchange(blocked, send_list):
    nrows, slot = send_list.shape
    me = lax.axis_index("rows")
    dests = (me + jnp.arange(nrows, dtype=jnp.int32)) % nrows
    wanted = jnp.take(send_list, dests, axis=0, mode="clip").reshape(-1)
    outgoing = jnp.take(blocked, wanted, axis=0, mode="clip")
    pieces = []
    for shift in range(1, nrows):
        chunk = outgoing[shift * slot:(shift + 1) * slot]
        pairs = [(i, (i + shift) % nrows) for i in range(nrows)]
        pieces.append(lax.ppermute(chunk, "rows", pairs))
    return outgoing[:slot], pieces


def row_sum(onehot, products):
    return jnp.einsum("bj,jkr->bkr", onehot, products, precision=lax.Precision.HIGHEST)


def products_of(sources, tiles):
    return jnp.einsum("jkc,jrc->jkr", sources, tiles, preferred_element_type=jnp.float32)


def first_apply(blocked, tile_vals, tile_row, tile_src, send_list):
    nblocks = blocked.shape[0]
    outgoing = jnp.take(blocked, send_list.reshape(-1), axis=0, mode="clip")
    incoming = lax.all_to_all(outgoing, "rows", 0, 0, tiled=True)
    sources = jnp.concatenate([blocked, incoming], axis=0)
    chosen = jnp.take(sources, tile_src.reshape(-1), axis=0, mode="clip")
    products = products_of(chosen, tile_vals)
    onehot = (tile_row.reshape(1, -1) == jnp.arange(nblocks, dtype=jnp.int32)[:, None]).astype(jnp.float32)
    return row_sum(onehot, products)


def sorted_apply(blocked, tiles_sorted, onehot, send_list):
    nblocks = blocked.shape[0]
    slot = send_list.shape[1]
    own_self, pieces = exchange(blocked, send_list)
    split = nblocks + slot
    own = products_of(jnp.concatenate([blocked, own_self], axis=0), tiles_sorted[:split])
    out = row_sum(onehot[:, :split], own)
    received = products_of(jnp.concatenate(pieces, axis=0), tiles_sorted[split:])
    return out + row_sum(onehot[:, split:], received)


def tree_sum_rows(value, nrows):
    step = 1
    while step < nrows:
        pairs = [(i, i ^ step) for i in range(nrows)]
        value = value + lax.ppermute(value, "rows", pairs)
        step *= 2
    return value


def gather_cols(piece, ncols):
    half = 2 if ncols % 2 == 0 else 1
    outer = ncols // half
    me = lax.axis_index("cols")
    parts, owners = [piece], [me]
    for shift in range(1, outer):
        pairs = [(i, (i + shift * half) % ncols) for i in range(ncols)]
        parts.append(lax.ppermute(piece, "cols", pairs))
        owners.append((me - shift * half) % ncols)
    if half == 2:
        pairs = [(i, i ^ 1) for i in range(ncols)]
        count = len(parts)
        for n in range(count):
            parts.append(lax.ppermute(parts[n], "cols", pairs))
            owners.append(owners[n] ^ 1)
    return parts, owners


def body(vectors, tile_vals, tile_row, tile_src, send_list, ritz_matrix):
    columns, length = vectors.shape
    side = tile_vals.shape[1]
    nblocks = length // side
    nrows = lax.axis_size("rows")
    ncols = lax.axis_size("cols")
    plan = plan_slots(tile_row, tile_src, send_list)
    start = vectors.reshape(columns, nblocks, side).transpose(1, 0, 2)
    first_pass = first_apply(start, tile_vals, tile_row, tile_src, send_list).astype(jnp.bfloat16)
    order, rowof, _ = plan
    tiles_sorted = jnp.take(tile_vals, order, axis=0, mode="clip")
    onehot = (rowof[None, :] == jnp.arange(nblocks, dtype=jnp.int32)[:, None]).astype(jnp.float32)
    second = sorted_apply(first_pass, tiles_sorted, onehot, send_list)
    filtered = (2.0 * second - start.astype(jnp.float32)).astype(jnp.bfloat16)
    total_nodes = length * nrows
    parts, owners = gather_cols(filtered, ncols)
    operated = sorted_apply(filtered, tiles_sorted, onehot, send_list).astype(jnp.bfloat16)
    contract = (((0, 2), (0, 2)), ((), ()))
    portion = jnp.concatenate(parts, axis=1)
    owner_ids = jnp.stack(owners).astype(jnp.int32)
    place = jnp.zeros((ncols,), jnp.int32).at[owner_ids].set(jnp.arange(ncols, dtype=jnp.int32))
    ritz_rows = ritz_matrix.reshape(ncols, columns, ritz_matrix.shape[1])
    weights = jnp.take(ritz_rows, owner_ids, axis=0, mode="clip").reshape(ritz_matrix.shape)
    turned = jnp.einsum("ij,bic->jbc", weights, portion, preferred_element_type=jnp.float32)
    rotated = turned.astype(jnp.bfloat16).reshape(ritz_matrix.shape[1], length)
    gram_rel = lax.dot_general(filtered, portion, contract, preferred_element_type=jnp.float32)
    proj_rel = lax.dot_general(operated, portion, contract, preferred_element_type=jnp.float32)
    both = jnp.stack([gram_rel, proj_rel]).reshape(2, columns, ncols, columns)
    both = jnp.take(both, place, axis=2, mode="clip").reshape(2, columns, ncols * columns)
    both = tree_sum_rows(both, nrows)
    gram_matrix = both[0] / total_nodes
    projected = both[1] / total_nodes
    return (rotated, gram_matrix, projected)


def solution(mesh):
    return jax.shard_map(
        body,
        mesh=mesh,
        in_specs=(
            P("cols", "rows"),
            P("rows", None, None),
            P("rows", None),
            P("rows", None),
            P("rows", None),
            P(None, "cols"),
        ),
        out_specs=(P("cols", "rows"), P("cols", None), P("cols", None)),
        check_vma=False,
    )
```

```python
import jax
import jax.numpy as jnp
from jax import lax
from jax.sharding import PartitionSpec as P


def plan_slots(tile_row, tile_src, send_list):
    nrows, slot = send_list.shape
    ntiles = tile_src.shape[-1]
    nblocks = ntiles - nrows * slot
    me = lax.axis_index("rows")
    src = tile_src.reshape(-1)
    peer = (src - nblocks) // slot
    shift = (me - peer) % nrows
    moved = nblocks + shift * slot + (src - nblocks) % slot
    slots = jnp.where(src < nblocks, src, moved)
    hit = slots[None, :] == jnp.arange(ntiles, dtype=jnp.int32)[:, None]
    tiles = jnp.arange(ntiles, dtype=jnp.int32)[None, :]
    order = jnp.sum(jnp.where(hit, tiles, 0), axis=1)
    rowof = jnp.sum(jnp.where(hit, tile_row.reshape(1, -1), 0), axis=1)
    return order, rowof, slots


def exchange(blocked, send_list):
    nrows, slot = send_list.shape
    me = lax.axis_index("rows")
    dests = (me + jnp.arange(nrows, dtype=jnp.int32)) % nrows
    wanted = jnp.take(send_list, dests, axis=0, mode="clip").reshape(-1)
    outgoing = jnp.take(blocked, wanted, axis=0, mode="clip")
    pieces = []
    for shift in range(1, nrows):
        chunk = outgoing[shift * slot:(shift + 1) * slot]
        pairs = [(i, (i + shift) % nrows) for i in range(nrows)]
        pieces.append(lax.ppermute(chunk, "rows", pairs))
    return outgoing[:slot], pieces


def row_sum(onehot, products):
    return jnp.einsum("bj,jkr->bkr", onehot, products, precision=lax.Precision.HIGHEST)


def products_of(sources, tiles):
    return jnp.einsum("jkc,jrc->jkr", sources, tiles, preferred_element_type=jnp.float32)


def first_apply(blocked, tile_vals, tile_row, tile_src, send_list):
    nblocks = blocked.shape[0]
    outgoing = jnp.take(blocked, send_list.reshape(-1), axis=0, mode="clip")
    incoming = lax.all_to_all(outgoing, "rows", 0, 0, tiled=True)
    sources = jnp.concatenate([blocked, incoming], axis=0)
    chosen = jnp.take(sources, tile_src.reshape(-1), axis=0, mode="clip")
    products = products_of(chosen, tile_vals)
    onehot = (tile_row.reshape(1, -1) == jnp.arange(nblocks, dtype=jnp.int32)[:, None]).astype(jnp.float32)
    return row_sum(onehot, products)


def sorted_apply(blocked, tiles_sorted, onehot, send_list):
    nblocks = blocked.shape[0]
    slot = send_list.shape[1]
    own_self, pieces = exchange(blocked, send_list)
    split = nblocks + slot
    own = products_of(jnp.concatenate([blocked, own_self], axis=0), tiles_sorted[:split])
    out = row_sum(onehot[:, :split], own)
    received = products_of(jnp.concatenate(pieces, axis=0), tiles_sorted[split:])
    return out + row_sum(onehot[:, split:], received)


def tree_sum_rows(value, nrows):
    step = 1
    while step < nrows:
        pairs = [(i, i ^ step) for i in range(nrows)]
        value = value + lax.ppermute(value, "rows", pairs)
        step *= 2
    return value


def gather_cols(piece, ncols):
    me = lax.axis_index("cols")
    parts, owners = [piece], [me]
    for shift in range(1, ncols):
        pairs = [(i, (i + shift) % ncols) for i in range(ncols)]
        parts.append(lax.ppermute(piece, "cols", pairs))
        owners.append((me - shift) % ncols)
    return parts, owners


def body(vectors, tile_vals, tile_row, tile_src, send_list, ritz_matrix):
    columns, length = vectors.shape
    side = tile_vals.shape[1]
    nblocks = length // side
    nrows = lax.axis_size("rows")
    ncols = lax.axis_size("cols")
    plan = plan_slots(tile_row, tile_src, send_list)
    start = vectors.reshape(columns, nblocks, side).transpose(1, 0, 2)
    first_pass = first_apply(start, tile_vals, tile_row, tile_src, send_list).astype(jnp.bfloat16)
    order, rowof, _ = plan
    tiles_sorted = jnp.take(tile_vals, order, axis=0, mode="clip")
    onehot = (rowof[None, :] == jnp.arange(nblocks, dtype=jnp.int32)[:, None]).astype(jnp.float32)
    second = sorted_apply(first_pass, tiles_sorted, onehot, send_list)
    filtered = (2.0 * second - start.astype(jnp.float32)).astype(jnp.bfloat16)
    total_nodes = length * nrows
    parts, owners = gather_cols(filtered, ncols)
    operated = sorted_apply(filtered, tiles_sorted, onehot, send_list).astype(jnp.bfloat16)
    contract = (((0, 2), (0, 2)), ((), ()))
    portion = jnp.concatenate(parts, axis=1)
    owner_ids = jnp.stack(owners).astype(jnp.int32)
    place = jnp.zeros((ncols,), jnp.int32).at[owner_ids].set(jnp.arange(ncols, dtype=jnp.int32))
    ritz_rows = ritz_matrix.reshape(ncols, columns, ritz_matrix.shape[1])
    weights = jnp.take(ritz_rows, owner_ids, axis=0, mode="clip").reshape(ritz_matrix.shape)
    turned = jnp.einsum("ij,bic->jbc", weights, portion, preferred_element_type=jnp.float32)
    rotated = turned.astype(jnp.bfloat16).reshape(ritz_matrix.shape[1], length)
    gram_rel = lax.dot_general(filtered, portion, contract, preferred_element_type=jnp.float32)
    proj_rel = lax.dot_general(operated, portion, contract, preferred_element_type=jnp.float32)
    both = jnp.stack([gram_rel, proj_rel]).reshape(2, columns, ncols, columns)
    both = jnp.take(both, place, axis=2, mode="clip").reshape(2, columns, ncols * columns)
    both = tree_sum_rows(both, nrows)
    gram_matrix = both[0] / total_nodes
    projected = both[1] / total_nodes
    return (rotated, gram_matrix, projected)


def solution(mesh):
    return jax.shard_map(
        body,
        mesh=mesh,
        in_specs=(
            P("cols", "rows"),
            P("rows", None, None),
            P("rows", None),
            P("rows", None),
            P("rows", None),
            P(None, "cols"),
        ),
        out_specs=(P("cols", "rows"), P("cols", None), P("cols", None)),
        check_vma=False,
    )
```

```python
import jax
import jax.numpy as jnp
from jax import lax
from jax.sharding import PartitionSpec as P


def plan_slots(tile_row, tile_src, send_list):
    nrows, slot = send_list.shape
    ntiles = tile_src.shape[-1]
    nblocks = ntiles - nrows * slot
    me = lax.axis_index("rows")
    src = tile_src.reshape(-1)
    peer = (src - nblocks) // slot
    shift = (me - peer) % nrows
    moved = nblocks + shift * slot + (src - nblocks) % slot
    slots = jnp.where(src < nblocks, src, moved)
    hit = slots[None, :] == jnp.arange(ntiles, dtype=jnp.int32)[:, None]
    tiles = jnp.arange(ntiles, dtype=jnp.int32)[None, :]
    order = jnp.sum(jnp.where(hit, tiles, 0), axis=1)
    rowof = jnp.sum(jnp.where(hit, tile_row.reshape(1, -1), 0), axis=1)
    return order, rowof, slots


def exchange(blocked, send_list):
    nrows, slot = send_list.shape
    me = lax.axis_index("rows")
    dests = (me + jnp.arange(nrows, dtype=jnp.int32)) % nrows
    wanted = jnp.take(send_list, dests, axis=0, mode="clip").reshape(-1)
    outgoing = jnp.take(blocked, wanted, axis=0, mode="clip")
    pieces = []
    for shift in range(1, nrows):
        chunk = outgoing[shift * slot:(shift + 1) * slot]
        pairs = [(i, (i + shift) % nrows) for i in range(nrows)]
        pieces.append(lax.ppermute(chunk, "rows", pairs))
    return outgoing[:slot], pieces


def row_sum(onehot, products):
    return jnp.einsum("bj,jkr->bkr", onehot, products, precision=lax.Precision.HIGHEST)


def products_of(sources, tiles):
    return jnp.einsum("jkc,jrc->jkr", sources, tiles, preferred_element_type=jnp.float32)


def first_apply(blocked, tile_vals, tile_row, tile_src, send_list):
    nblocks = blocked.shape[0]
    outgoing = jnp.take(blocked, send_list.reshape(-1), axis=0, mode="clip")
    incoming = lax.all_to_all(outgoing, "rows", 0, 0, tiled=True)
    sources = jnp.concatenate([blocked, incoming], axis=0)
    chosen = jnp.take(sources, tile_src.reshape(-1), axis=0, mode="clip")
    products = products_of(chosen, tile_vals)
    onehot = (tile_row.reshape(1, -1) == jnp.arange(nblocks, dtype=jnp.int32)[:, None]).astype(jnp.float32)
    return row_sum(onehot, products)


def sorted_apply(blocked, tiles_sorted, onehot, send_list):
    nblocks = blocked.shape[0]
    slot = send_list.shape[1]
    own_self, pieces = exchange(blocked, send_list)
    split = nblocks + slot
    own = products_of(jnp.concatenate([blocked, own_self], axis=0), tiles_sorted[:split])
    out = row_sum(onehot[:, :split], own)
    received = products_of(jnp.concatenate(pieces, axis=0), tiles_sorted[split:])
    return out + row_sum(onehot[:, split:], received)


def tree_sum_rows(value, nrows):
    step = 1
    while step < nrows:
        pairs = [(i, i ^ step) for i in range(nrows)]
        value = value + lax.ppermute(value, "rows", pairs)
        step *= 2
    return value


def gather_cols(piece, ncols):
    me = lax.axis_index("cols")
    parts, owners = [piece], [me]
    for shift in range(1, ncols):
        pairs = [(i, (i + shift) % ncols) for i in range(ncols)]
        parts.append(lax.ppermute(piece, "cols", pairs))
        owners.append((me - shift) % ncols)
    return parts, owners


def body(vectors, tile_vals, tile_row, tile_src, send_list, ritz_matrix):
    columns, length = vectors.shape
    side = tile_vals.shape[1]
    nblocks = length // side
    nrows = lax.axis_size("rows")
    ncols = lax.axis_size("cols")
    plan = plan_slots(tile_row, tile_src, send_list)
    start = vectors.reshape(columns, nblocks, side).transpose(1, 0, 2)
    first_pass = first_apply(start, tile_vals, tile_row, tile_src, send_list).astype(jnp.bfloat16)
    order, rowof, _ = plan
    tiles_sorted = jnp.take(tile_vals, order, axis=0, mode="clip")
    onehot = (rowof[None, :] == jnp.arange(nblocks, dtype=jnp.int32)[:, None]).astype(jnp.float32)
    second = sorted_apply(first_pass, tiles_sorted, onehot, send_list)
    filtered = (2.0 * second - start.astype(jnp.float32)).astype(jnp.bfloat16)
    total_nodes = length * nrows
    parts, owners = gather_cols(filtered, ncols)
    operated = sorted_apply(filtered, tiles_sorted, onehot, send_list).astype(jnp.bfloat16)
    contract = (((0, 2), (0, 2)), ((), ()))
    portion = jnp.concatenate(parts, axis=1)
    owner_ids = jnp.stack(owners).astype(jnp.int32)
    place = jnp.zeros((ncols,), jnp.int32).at[owner_ids].set(jnp.arange(ncols, dtype=jnp.int32))
    ritz_rows = ritz_matrix.reshape(ncols, columns, ritz_matrix.shape[1])
    weights = jnp.take(ritz_rows, owner_ids, axis=0, mode="clip").reshape(ritz_matrix.shape)
    turned = jnp.einsum("ij,bic->jbc", weights, portion, preferred_element_type=jnp.float32)
    rotated = turned.astype(jnp.bfloat16).reshape(ritz_matrix.shape[1], length)
    lhs = jnp.concatenate([filtered, operated], axis=1)
    both = lax.dot_general(lhs, portion, contract, preferred_element_type=jnp.float32)
    both = both.reshape(2, columns, ncols, columns)
    both = jnp.take(both, place, axis=2, mode="clip").reshape(2, columns, ncols * columns)
    both = tree_sum_rows(both, nrows)
    gram_matrix = both[0] / total_nodes
    projected = both[1] / total_nodes
    return (rotated, gram_matrix, projected)


def solution(mesh):
    return jax.shard_map(
        body,
        mesh=mesh,
        in_specs=(
            P("cols", "rows"),
            P("rows", None, None),
            P("rows", None),
            P("rows", None),
            P("rows", None),
            P(None, "cols"),
        ),
        out_specs=(P("cols", "rows"), P("cols", None), P("cols", None)),
        check_vma=False,
    )
```

```python
import jax
import jax.numpy as jnp
from jax import lax
from jax.sharding import PartitionSpec as P


def plan_slots(tile_row, tile_src, send_list):
    nrows, slot = send_list.shape
    ntiles = tile_src.shape[-1]
    nblocks = ntiles - nrows * slot
    me = lax.axis_index("rows")
    src = tile_src.reshape(-1)
    peer = (src - nblocks) // slot
    shift = (me - peer) % nrows
    moved = nblocks + shift * slot + (src - nblocks) % slot
    slots = jnp.where(src < nblocks, src, moved)
    hit = slots[None, :] == jnp.arange(ntiles, dtype=jnp.int32)[:, None]
    tiles = jnp.arange(ntiles, dtype=jnp.int32)[None, :]
    order = jnp.sum(jnp.where(hit, tiles, 0), axis=1)
    rowof = jnp.sum(jnp.where(hit, tile_row.reshape(1, -1), 0), axis=1)
    return order, rowof, slots


def exchange(blocked, send_list):
    nrows, slot = send_list.shape
    me = lax.axis_index("rows")
    dests = (me + jnp.arange(nrows, dtype=jnp.int32)) % nrows
    wanted = jnp.take(send_list, dests, axis=0, mode="clip").reshape(-1)
    outgoing = jnp.take(blocked, wanted, axis=0, mode="clip")
    pieces = []
    for shift in range(1, nrows):
        chunk = outgoing[shift * slot:(shift + 1) * slot]
        pairs = [(i, (i + shift) % nrows) for i in range(nrows)]
        pieces.append(lax.ppermute(chunk, "rows", pairs))
    return outgoing[:slot], pieces


def row_sum(onehot, products):
    return jnp.einsum("bj,jkr->bkr", onehot, products, precision=lax.Precision.HIGHEST)


def products_of(sources, tiles):
    return jnp.einsum("jkc,jrc->jkr", sources, tiles, preferred_element_type=jnp.float32)


def first_apply(blocked, tiles_sorted, onehot, send_list):
    nblocks = blocked.shape[0]
    nrows, slot = send_list.shape
    me = lax.axis_index("rows")
    outgoing = jnp.take(blocked, send_list.reshape(-1), axis=0, mode="clip")
    incoming = lax.all_to_all(outgoing, "rows", 0, 0, tiled=True)
    mine = lax.dynamic_index_in_dim(send_list, me, 0, keepdims=False)
    own_self = jnp.take(blocked, mine, axis=0, mode="clip")
    split = nblocks + slot
    own = products_of(jnp.concatenate([blocked, own_self], axis=0), tiles_sorted[:split])
    out = row_sum(onehot[:, :split], own)
    shifts = jnp.arange(1, nrows, dtype=jnp.int32)[:, None]
    picks = (((me - shifts) % nrows) * slot + jnp.arange(slot, dtype=jnp.int32)[None, :]).reshape(-1)
    received = products_of(jnp.take(incoming, picks, axis=0, mode="clip"), tiles_sorted[split:])
    return out + row_sum(onehot[:, split:], received)


def sorted_apply(blocked, tiles_sorted, onehot, send_list):
    nblocks = blocked.shape[0]
    slot = send_list.shape[1]
    own_self, pieces = exchange(blocked, send_list)
    split = nblocks + slot
    own = products_of(jnp.concatenate([blocked, own_self], axis=0), tiles_sorted[:split])
    out = row_sum(onehot[:, :split], own)
    received = products_of(jnp.concatenate(pieces, axis=0), tiles_sorted[split:])
    return out + row_sum(onehot[:, split:], received)


def tree_sum_rows(value, nrows):
    step = 1
    while step < nrows:
        pairs = [(i, i ^ step) for i in range(nrows)]
        value = value + lax.ppermute(value, "rows", pairs)
        step *= 2
    return value


def gather_cols(piece, ncols):
    me = lax.axis_index("cols")
    parts, owners = [piece], [me]
    for shift in range(1, ncols):
        pairs = [(i, (i + shift) % ncols) for i in range(ncols)]
        parts.append(lax.ppermute(piece, "cols", pairs))
        owners.append((me - shift) % ncols)
    return parts, owners


def body(vectors, tile_vals, tile_row, tile_src, send_list, ritz_matrix):
    columns, length = vectors.shape
    side = tile_vals.shape[1]
    nblocks = length // side
    nrows = lax.axis_size("rows")
    ncols = lax.axis_size("cols")
    plan = plan_slots(tile_row, tile_src, send_list)
    start = vectors.reshape(columns, nblocks, side).transpose(1, 0, 2)
    order, rowof, _ = plan
    tiles_sorted = jnp.take(tile_vals, order, axis=0, mode="clip")
    onehot = (rowof[None, :] == jnp.arange(nblocks, dtype=jnp.int32)[:, None]).astype(jnp.float32)
    first_pass = first_apply(start, tiles_sorted, onehot, send_list).astype(jnp.bfloat16)
    second = sorted_apply(first_pass, tiles_sorted, onehot, send_list)
    filtered = (2.0 * second - start.astype(jnp.float32)).astype(jnp.bfloat16)
    total_nodes = length * nrows
    parts, owners = gather_cols(filtered, ncols)
    operated = sorted_apply(filtered, tiles_sorted, onehot, send_list).astype(jnp.bfloat16)
    contract = (((0, 2), (0, 2)), ((), ()))
    portion = jnp.concatenate(parts, axis=1)
    owner_ids = jnp.stack(owners).astype(jnp.int32)
    place = jnp.zeros((ncols,), jnp.int32).at[owner_ids].set(jnp.arange(ncols, dtype=jnp.int32))
    ritz_rows = ritz_matrix.reshape(ncols, columns, ritz_matrix.shape[1])
    weights = jnp.take(ritz_rows, owner_ids, axis=0, mode="clip").reshape(ritz_matrix.shape)
    turned = jnp.einsum("ij,bic->jbc", weights, portion, preferred_element_type=jnp.float32)
    rotated = turned.astype(jnp.bfloat16).reshape(ritz_matrix.shape[1], length)
    lhs = jnp.concatenate([filtered, operated], axis=1)
    both = lax.dot_general(lhs, portion, contract, preferred_element_type=jnp.float32)
    both = both.reshape(2, columns, ncols, columns)
    both = jnp.take(both, place, axis=2, mode="clip").reshape(2, columns, ncols * columns)
    both = tree_sum_rows(both, nrows)
    gram_matrix = both[0] / total_nodes
    projected = both[1] / total_nodes
    return (rotated, gram_matrix, projected)


def solution(mesh):
    return jax.shard_map(
        body,
        mesh=mesh,
        in_specs=(
            P("cols", "rows"),
            P("rows", None, None),
            P("rows", None),
            P("rows", None),
            P("rows", None),
            P(None, "cols"),
        ),
        out_specs=(P("cols", "rows"), P("cols", None), P("cols", None)),
        check_vma=False,
    )
```

```python
import jax
import jax.numpy as jnp
from jax import lax
from jax.sharding import PartitionSpec as P


def plan_slots(tile_row, tile_src, send_list):
    nrows, slot = send_list.shape
    ntiles = tile_src.shape[-1]
    nblocks = ntiles - nrows * slot
    me = lax.axis_index("rows")
    src = tile_src.reshape(-1)
    peer = (src - nblocks) // slot
    shift = (me - peer) % nrows
    moved = nblocks + shift * slot + (src - nblocks) % slot
    slots = jnp.where(src < nblocks, src, moved)
    hit = slots[None, :] == jnp.arange(ntiles, dtype=jnp.int32)[:, None]
    tiles = jnp.arange(ntiles, dtype=jnp.int32)[None, :]
    order = jnp.sum(jnp.where(hit, tiles, 0), axis=1)
    rowof = jnp.sum(jnp.where(hit, tile_row.reshape(1, -1), 0), axis=1)
    return order, rowof, slots


def exchange(blocked, send_list):
    nrows, slot = send_list.shape
    me = lax.axis_index("rows")
    dests = (me + jnp.arange(nrows, dtype=jnp.int32)) % nrows
    wanted = jnp.take(send_list, dests, axis=0, mode="clip").reshape(-1)
    outgoing = jnp.take(blocked, wanted, axis=0, mode="clip")
    pieces = []
    for shift in range(1, nrows):
        chunk = outgoing[shift * slot:(shift + 1) * slot]
        pairs = [(i, (i + shift) % nrows) for i in range(nrows)]
        pieces.append(lax.ppermute(chunk, "rows", pairs))
    return outgoing[:slot], pieces


def row_sum(onehot, products):
    return jnp.einsum("bj,jkr->bkr", onehot, products, precision=lax.Precision.HIGHEST)


def products_of(sources, tiles):
    return jnp.einsum("jkc,jrc->jkr", sources, tiles, preferred_element_type=jnp.float32)


def first_apply(blocked, tile_vals, tile_row, tile_src, send_list):
    nblocks = blocked.shape[0]
    outgoing = jnp.take(blocked, send_list.reshape(-1), axis=0, mode="clip")
    incoming = lax.all_to_all(outgoing, "rows", 0, 0, tiled=True)
    sources = jnp.concatenate([blocked, incoming], axis=0)
    chosen = jnp.take(sources, tile_src.reshape(-1), axis=0, mode="clip")
    products = products_of(chosen, tile_vals)
    onehot = (tile_row.reshape(1, -1) == jnp.arange(nblocks, dtype=jnp.int32)[:, None]).astype(jnp.float32)
    return row_sum(onehot, products)


def sorted_apply(blocked, tiles_sorted, onehot, send_list):
    nblocks = blocked.shape[0]
    slot = send_list.shape[1]
    own_self, pieces = exchange(blocked, send_list)
    split = nblocks + slot
    own = products_of(jnp.concatenate([blocked, own_self], axis=0), tiles_sorted[:split])
    out = row_sum(onehot[:, :split], own)
    received = products_of(jnp.concatenate(pieces, axis=0), tiles_sorted[split:])
    return out + row_sum(onehot[:, split:], received)


def tree_sum_rows(value, nrows):
    step = 1
    while step < nrows:
        pairs = [(i, i ^ step) for i in range(nrows)]
        value = value + lax.ppermute(value, "rows", pairs)
        step *= 2
    return value


def gather_cols(piece, ncols):
    me = lax.axis_index("cols")
    parts, owners = [piece], [me]
    for shift in range(1, ncols):
        pairs = [(i, (i + shift) % ncols) for i in range(ncols)]
        parts.append(lax.ppermute(piece, "cols", pairs))
        owners.append((me - shift) % ncols)
    return parts, owners


def body(vectors, tile_vals, tile_row, tile_src, send_list, ritz_matrix):
    columns, length = vectors.shape
    side = tile_vals.shape[1]
    nblocks = length // side
    nrows = lax.axis_size("rows")
    ncols = lax.axis_size("cols")
    plan = plan_slots(tile_row, tile_src, send_list)
    start = vectors.reshape(columns, nblocks, side).transpose(1, 0, 2)
    first_pass = first_apply(start, tile_vals, tile_row, tile_src, send_list).astype(jnp.bfloat16)
    order, rowof, _ = plan
    tiles_sorted = jnp.take(tile_vals, order, axis=0, mode="clip")
    onehot = (rowof[None, :] == jnp.arange(nblocks, dtype=jnp.int32)[:, None]).astype(jnp.float32)
    second = sorted_apply(first_pass, tiles_sorted, onehot, send_list)
    filtered = (2.0 * second - start.astype(jnp.float32)).astype(jnp.bfloat16)
    total_nodes = length * nrows
    spread = jnp.broadcast_to(filtered[None], (ncols,) + filtered.shape)
    gathered = lax.all_to_all(spread, "cols", 0, 0, tiled=False)
    operated = sorted_apply(filtered, tiles_sorted, onehot, send_list).astype(jnp.bfloat16)
    ritz_rows = ritz_matrix.reshape(ncols, columns, ritz_matrix.shape[1])
    turned = jnp.einsum("mij,mbic->jbc", ritz_rows, gathered, preferred_element_type=jnp.float32)
    rotated = turned.astype(jnp.bfloat16).reshape(ritz_matrix.shape[1], length)
    lhs = jnp.concatenate([filtered, operated], axis=1)
    both = jnp.einsum("bsc,mbjc->smj", lhs, gathered, preferred_element_type=jnp.float32)
    both = both.reshape(2, columns, ncols * columns)
    both = tree_sum_rows(both, nrows)
    gram_matrix = both[0] / total_nodes
    projected = both[1] / total_nodes
    return (rotated, gram_matrix, projected)


def solution(mesh):
    return jax.shard_map(
        body,
        mesh=mesh,
        in_specs=(
            P("cols", "rows"),
            P("rows", None, None),
            P("rows", None),
            P("rows", None),
            P("rows", None),
            P(None, "cols"),
        ),
        out_specs=(P("cols", "rows"), P("cols", None), P("cols", None)),
        check_vma=False,
    )
```

```python
import jax
import jax.numpy as jnp
from jax import lax
from jax.sharding import PartitionSpec as P


def plan_slots(tile_row, tile_src, send_list):
    nrows, slot = send_list.shape
    ntiles = tile_src.shape[-1]
    nblocks = ntiles - nrows * slot
    me = lax.axis_index("rows")
    src = tile_src.reshape(-1)
    peer = (src - nblocks) // slot
    shift = (me - peer) % nrows
    moved = nblocks + shift * slot + (src - nblocks) % slot
    slots = jnp.where(src < nblocks, src, moved)
    hit = slots[None, :] == jnp.arange(ntiles, dtype=jnp.int32)[:, None]
    tiles = jnp.arange(ntiles, dtype=jnp.int32)[None, :]
    order = jnp.sum(jnp.where(hit, tiles, 0), axis=1)
    rowof = jnp.sum(jnp.where(hit, tile_row.reshape(1, -1), 0), axis=1)
    return order, rowof, slots


def exchange(blocked, send_list):
    nrows, slot = send_list.shape
    me = lax.axis_index("rows")
    dests = (me + jnp.arange(nrows, dtype=jnp.int32)) % nrows
    wanted = jnp.take(send_list, dests, axis=0, mode="clip").reshape(-1)
    outgoing = jnp.take(blocked, wanted, axis=0, mode="clip")
    pieces = []
    for shift in range(1, nrows):
        chunk = outgoing[shift * slot:(shift + 1) * slot]
        pairs = [(i, (i + shift) % nrows) for i in range(nrows)]
        pieces.append(lax.ppermute(chunk, "rows", pairs))
    return outgoing[:slot], pieces


def row_sum(onehot, products):
    return jnp.einsum("bj,jkr->bkr", onehot, products, precision=lax.Precision.HIGH)


def products_of(sources, tiles):
    return jnp.einsum("jkc,jrc->jkr", sources, tiles, preferred_element_type=jnp.float32)


def first_apply(blocked, tile_vals, tile_row, tile_src, send_list):
    nblocks = blocked.shape[0]
    outgoing = jnp.take(blocked, send_list.reshape(-1), axis=0, mode="clip")
    incoming = lax.all_to_all(outgoing, "rows", 0, 0, tiled=True)
    sources = jnp.concatenate([blocked, incoming], axis=0)
    chosen = jnp.take(sources, tile_src.reshape(-1), axis=0, mode="clip")
    products = products_of(chosen, tile_vals)
    onehot = (tile_row.reshape(1, -1) == jnp.arange(nblocks, dtype=jnp.int32)[:, None]).astype(jnp.float32)
    return row_sum(onehot, products)


def sorted_apply(blocked, tiles_sorted, onehot, send_list):
    nblocks = blocked.shape[0]
    slot = send_list.shape[1]
    own_self, pieces = exchange(blocked, send_list)
    split = nblocks + slot
    own = products_of(jnp.concatenate([blocked, own_self], axis=0), tiles_sorted[:split])
    out = row_sum(onehot[:, :split], own)
    received = products_of(jnp.concatenate(pieces, axis=0), tiles_sorted[split:])
    return out + row_sum(onehot[:, split:], received)


def tree_sum_rows(value, nrows):
    step = 1
    while step < nrows:
        pairs = [(i, i ^ step) for i in range(nrows)]
        value = value + lax.ppermute(value, "rows", pairs)
        step *= 2
    return value


def gather_cols(piece, ncols):
    me = lax.axis_index("cols")
    parts, owners = [piece], [me]
    for shift in range(1, ncols):
        pairs = [(i, (i + shift) % ncols) for i in range(ncols)]
        parts.append(lax.ppermute(piece, "cols", pairs))
        owners.append((me - shift) % ncols)
    return parts, owners


def body(vectors, tile_vals, tile_row, tile_src, send_list, ritz_matrix):
    columns, length = vectors.shape
    side = tile_vals.shape[1]
    nblocks = length // side
    nrows = lax.axis_size("rows")
    ncols = lax.axis_size("cols")
    plan = plan_slots(tile_row, tile_src, send_list)
    start = vectors.reshape(columns, nblocks, side).transpose(1, 0, 2)
    first_pass = first_apply(start, tile_vals, tile_row, tile_src, send_list).astype(jnp.bfloat16)
    order, rowof, _ = plan
    tiles_sorted = jnp.take(tile_vals, order, axis=0, mode="clip")
    onehot = (rowof[None, :] == jnp.arange(nblocks, dtype=jnp.int32)[:, None]).astype(jnp.float32)
    second = sorted_apply(first_pass, tiles_sorted, onehot, send_list)
    filtered = (2.0 * second - start.astype(jnp.float32)).astype(jnp.bfloat16)
    total_nodes = length * nrows
    parts, owners = gather_cols(filtered, ncols)
    operated = sorted_apply(filtered, tiles_sorted, onehot, send_list).astype(jnp.bfloat16)
    contract = (((0, 2), (0, 2)), ((), ()))
    portion = jnp.concatenate(parts, axis=1)
    owner_ids = jnp.stack(owners).astype(jnp.int32)
    place = jnp.zeros((ncols,), jnp.int32).at[owner_ids].set(jnp.arange(ncols, dtype=jnp.int32))
    ritz_rows = ritz_matrix.reshape(ncols, columns, ritz_matrix.shape[1])
    weights = jnp.take(ritz_rows, owner_ids, axis=0, mode="clip").reshape(ritz_matrix.shape)
    turned = jnp.einsum("ij,bic->jbc", weights, portion, preferred_element_type=jnp.float32)
    rotated = turned.astype(jnp.bfloat16).reshape(ritz_matrix.shape[1], length)
    lhs = jnp.concatenate([filtered, operated], axis=1)
    both = lax.dot_general(lhs, portion, contract, preferred_element_type=jnp.float32)
    both = both.reshape(2, columns, ncols, columns)
    both = jnp.take(both, place, axis=2, mode="clip").reshape(2, columns, ncols * columns)
    both = tree_sum_rows(both, nrows)
    gram_matrix = both[0] / total_nodes
    projected = both[1] / total_nodes
    return (rotated, gram_matrix, projected)


def solution(mesh):
    return jax.shard_map(
        body,
        mesh=mesh,
        in_specs=(
            P("cols", "rows"),
            P("rows", None, None),
            P("rows", None),
            P("rows", None),
            P("rows", None),
            P(None, "cols"),
        ),
        out_specs=(P("cols", "rows"), P("cols", None), P("cols", None)),
        check_vma=False,
    )
```

```python
import jax
import jax.numpy as jnp
from jax import lax
from jax.sharding import PartitionSpec as P


def plan_slots(tile_row, tile_src, send_list):
    nrows, slot = send_list.shape
    ntiles = tile_src.shape[-1]
    nblocks = ntiles - nrows * slot
    me = lax.axis_index("rows")
    src = tile_src.reshape(-1)
    peer = (src - nblocks) // slot
    shift = (me - peer) % nrows
    moved = nblocks + shift * slot + (src - nblocks) % slot
    slots = jnp.where(src < nblocks, src, moved)
    hit = slots[None, :] == jnp.arange(ntiles, dtype=jnp.int32)[:, None]
    tiles = jnp.arange(ntiles, dtype=jnp.int32)[None, :]
    order = jnp.sum(jnp.where(hit, tiles, 0), axis=1)
    rowof = jnp.sum(jnp.where(hit, tile_row.reshape(1, -1), 0), axis=1)
    return order, rowof, slots


def exchange(blocked, send_list):
    nrows, slot = send_list.shape
    me = lax.axis_index("rows")
    dests = (me + jnp.arange(nrows, dtype=jnp.int32)) % nrows
    wanted = jnp.take(send_list, dests, axis=0, mode="clip").reshape(-1)
    outgoing = jnp.take(blocked, wanted, axis=0, mode="clip")
    pieces = []
    for shift in range(1, nrows):
        chunk = outgoing[shift * slot:(shift + 1) * slot]
        pairs = [(i, (i + shift) % nrows) for i in range(nrows)]
        pieces.append(lax.ppermute(chunk, "rows", pairs))
    return outgoing[:slot], pieces


def row_sum(onehot, products):
    return jnp.einsum("bj,jkr->bkr", onehot, products, precision=lax.Precision.HIGH)


def products_of(sources, tiles):
    return jnp.einsum("jkc,jrc->jkr", sources, tiles, preferred_element_type=jnp.float32)


def first_apply(blocked, tile_vals, tile_row, tile_src, send_list):
    nblocks = blocked.shape[0]
    outgoing = jnp.take(blocked, send_list.reshape(-1), axis=0, mode="clip")
    incoming = lax.all_to_all(outgoing, "rows", 0, 0, tiled=True)
    sources = jnp.concatenate([blocked, incoming], axis=0)
    chosen = jnp.take(sources, tile_src.reshape(-1), axis=0, mode="clip")
    products = products_of(chosen, tile_vals)
    onehot = (tile_row.reshape(1, -1) == jnp.arange(nblocks, dtype=jnp.int32)[:, None]).astype(jnp.float32)
    return row_sum(onehot, products)


def sorted_apply(blocked, tiles_sorted, onehot, send_list):
    nblocks = blocked.shape[0]
    slot = send_list.shape[1]
    own_self, pieces = exchange(blocked, send_list)
    split = nblocks + slot
    own = products_of(jnp.concatenate([blocked, own_self], axis=0), tiles_sorted[:split])
    out = row_sum(onehot[:, :split], own)
    received = products_of(jnp.concatenate(pieces, axis=0), tiles_sorted[split:])
    return out + row_sum(onehot[:, split:], received)


def tree_sum_rows(value, nrows):
    step = 1
    if nrows % 2 == 0 and nrows <= 8:
        value = value + lax.ppermute(value, "rows", [(i, i ^ 1) for i in range(nrows)])
        groups = nrows // 2
        me = lax.axis_index("rows") // 2
        got = [value]
        for shift in range(1, groups):
            pairs = [(i, (i + 2 * shift) % nrows) for i in range(nrows)]
            got.append(lax.ppermute(value, "rows", pairs))
        owners = (me - jnp.arange(groups, dtype=jnp.int32)) % groups
        place = jnp.zeros((groups,), jnp.int32).at[owners].set(jnp.arange(groups, dtype=jnp.int32))
        ordered = jnp.take(jnp.stack(got), place, axis=0, mode="clip")
        total = ordered[0]
        for n in range(1, groups):
            total = total + ordered[n]
        return total
    while step < nrows:
        pairs = [(i, i ^ step) for i in range(nrows)]
        value = value + lax.ppermute(value, "rows", pairs)
        step *= 2
    return value


def gather_cols(piece, ncols):
    me = lax.axis_index("cols")
    parts, owners = [piece], [me]
    for shift in range(1, ncols):
        pairs = [(i, (i + shift) % ncols) for i in range(ncols)]
        parts.append(lax.ppermute(piece, "cols", pairs))
        owners.append((me - shift) % ncols)
    return parts, owners


def body(vectors, tile_vals, tile_row, tile_src, send_list, ritz_matrix):
    columns, length = vectors.shape
    side = tile_vals.shape[1]
    nblocks = length // side
    nrows = lax.axis_size("rows")
    ncols = lax.axis_size("cols")
    plan = plan_slots(tile_row, tile_src, send_list)
    start = vectors.reshape(columns, nblocks, side).transpose(1, 0, 2)
    first_pass = first_apply(start, tile_vals, tile_row, tile_src, send_list).astype(jnp.bfloat16)
    order, rowof, _ = plan
    tiles_sorted = jnp.take(tile_vals, order, axis=0, mode="clip")
    onehot = (rowof[None, :] == jnp.arange(nblocks, dtype=jnp.int32)[:, None]).astype(jnp.float32)
    second = sorted_apply(first_pass, tiles_sorted, onehot, send_list)
    filtered = (2.0 * second - start.astype(jnp.float32)).astype(jnp.bfloat16)
    total_nodes = length * nrows
    parts, owners = gather_cols(filtered, ncols)
    operated = sorted_apply(filtered, tiles_sorted, onehot, send_list).astype(jnp.bfloat16)
    contract = (((0, 2), (0, 2)), ((), ()))
    portion = jnp.concatenate(parts, axis=1)
    owner_ids = jnp.stack(owners).astype(jnp.int32)
    place = jnp.zeros((ncols,), jnp.int32).at[owner_ids].set(jnp.arange(ncols, dtype=jnp.int32))
    ritz_rows = ritz_matrix.reshape(ncols, columns, ritz_matrix.shape[1])
    weights = jnp.take(ritz_rows, owner_ids, axis=0, mode="clip").reshape(ritz_matrix.shape)
    turned = jnp.einsum("ij,bic->jbc", weights, portion, preferred_element_type=jnp.float32)
    rotated = turned.astype(jnp.bfloat16).reshape(ritz_matrix.shape[1], length)
    lhs = jnp.concatenate([filtered, operated], axis=1)
    both = lax.dot_general(lhs, portion, contract, preferred_element_type=jnp.float32)
    both = both.reshape(2, columns, ncols, columns)
    both = jnp.take(both, place, axis=2, mode="clip").reshape(2, columns, ncols * columns)
    both = tree_sum_rows(both, nrows)
    gram_matrix = both[0] / total_nodes
    projected = both[1] / total_nodes
    return (rotated, gram_matrix, projected)


def solution(mesh):
    return jax.shard_map(
        body,
        mesh=mesh,
        in_specs=(
            P("cols", "rows"),
            P("rows", None, None),
            P("rows", None),
            P("rows", None),
            P("rows", None),
            P(None, "cols"),
        ),
        out_specs=(P("cols", "rows"), P("cols", None), P("cols", None)),
        check_vma=False,
    )
```

```python
import jax
import jax.numpy as jnp
from jax import lax
from jax.sharding import PartitionSpec as P


def plan_slots(tile_row, tile_src, send_list):
    nrows, slot = send_list.shape
    ntiles = tile_src.shape[-1]
    nblocks = ntiles - nrows * slot
    me = lax.axis_index("rows")
    src = tile_src.reshape(-1)
    peer = (src - nblocks) // slot
    shift = (me - peer) % nrows
    moved = nblocks + shift * slot + (src - nblocks) % slot
    slots = jnp.where(src < nblocks, src, moved)
    hit = slots[None, :] == jnp.arange(ntiles, dtype=jnp.int32)[:, None]
    tiles = jnp.arange(ntiles, dtype=jnp.int32)[None, :]
    order = jnp.sum(jnp.where(hit, tiles, 0), axis=1)
    rowof = jnp.sum(jnp.where(hit, tile_row.reshape(1, -1), 0), axis=1)
    return order, rowof, slots


def exchange(blocked, send_list):
    nrows, slot = send_list.shape
    me = lax.axis_index("rows")
    dests = (me + jnp.arange(nrows, dtype=jnp.int32)) % nrows
    wanted = jnp.take(send_list, dests, axis=0, mode="clip").reshape(-1)
    outgoing = jnp.take(blocked, wanted, axis=0, mode="clip")
    pieces = []
    for shift in range(1, nrows):
        chunk = outgoing[shift * slot:(shift + 1) * slot]
        pairs = [(i, (i + shift) % nrows) for i in range(nrows)]
        pieces.append(lax.ppermute(chunk, "rows", pairs))
    return outgoing[:slot], pieces


def row_sum(onehot, products):
    return jnp.einsum("bj,jkr->bkr", onehot, products, precision=lax.Precision.HIGH)


def products_of(sources, tiles):
    return jnp.einsum("jkc,jrc->jkr", sources, tiles, preferred_element_type=jnp.float32)


def first_apply(blocked, tiles_sorted, onehot, send_list):
    nrows, slot = send_list.shape
    me = lax.axis_index("rows")
    outgoing = jnp.take(blocked, send_list.reshape(-1), axis=0, mode="clip")
    incoming = lax.all_to_all(outgoing, "rows", 0, 0, tiled=True)
    mine = lax.dynamic_index_in_dim(send_list, me, 0, keepdims=False)
    own_self = jnp.take(blocked, mine, axis=0, mode="clip")
    shifts = jnp.arange(1, nrows, dtype=jnp.int32)[:, None]
    picks = (((me - shifts) % nrows) * slot + jnp.arange(slot, dtype=jnp.int32)[None, :]).reshape(-1)
    received = jnp.take(incoming, picks, axis=0, mode="clip")
    sources = jnp.concatenate([blocked, own_self, received], axis=0)
    return row_sum(onehot, products_of(sources, tiles_sorted))


def sorted_apply(blocked, tiles_sorted, onehot, send_list):
    nblocks = blocked.shape[0]
    slot = send_list.shape[1]
    own_self, pieces = exchange(blocked, send_list)
    split = nblocks + slot
    own = products_of(jnp.concatenate([blocked, own_self], axis=0), tiles_sorted[:split])
    out = row_sum(onehot[:, :split], own)
    received = products_of(jnp.concatenate(pieces, axis=0), tiles_sorted[split:])
    return out + row_sum(onehot[:, split:], received)


def tree_sum_rows(value, nrows):
    step = 1
    if nrows % 2 == 0 and nrows <= 8:
        value = value + lax.ppermute(value, "rows", [(i, i ^ 1) for i in range(nrows)])
        groups = nrows // 2
        me = lax.axis_index("rows") // 2
        got = [value]
        for shift in range(1, groups):
            pairs = [(i, (i + 2 * shift) % nrows) for i in range(nrows)]
            got.append(lax.ppermute(value, "rows", pairs))
        owners = (me - jnp.arange(groups, dtype=jnp.int32)) % groups
        place = jnp.zeros((groups,), jnp.int32).at[owners].set(jnp.arange(groups, dtype=jnp.int32))
        ordered = jnp.take(jnp.stack(got), place, axis=0, mode="clip")
        total = ordered[0]
        for n in range(1, groups):
            total = total + ordered[n]
        return total
    while step < nrows:
        pairs = [(i, i ^ step) for i in range(nrows)]
        value = value + lax.ppermute(value, "rows", pairs)
        step *= 2
    return value


def gather_cols(piece, ncols):
    me = lax.axis_index("cols")
    parts, owners = [piece], [me]
    for shift in range(1, ncols):
        pairs = [(i, (i + shift) % ncols) for i in range(ncols)]
        parts.append(lax.ppermute(piece, "cols", pairs))
        owners.append((me - shift) % ncols)
    return parts, owners


def body(vectors, tile_vals, tile_row, tile_src, send_list, ritz_matrix):
    columns, length = vectors.shape
    side = tile_vals.shape[1]
    nblocks = length // side
    nrows = lax.axis_size("rows")
    ncols = lax.axis_size("cols")
    plan = plan_slots(tile_row, tile_src, send_list)
    start = vectors.reshape(columns, nblocks, side).transpose(1, 0, 2)
    order, rowof, _ = plan
    tiles_sorted = jnp.take(tile_vals, order, axis=0, mode="clip")
    onehot = (rowof[None, :] == jnp.arange(nblocks, dtype=jnp.int32)[:, None]).astype(jnp.float32)
    first_pass = first_apply(start, tiles_sorted, onehot, send_list).astype(jnp.bfloat16)
    second = sorted_apply(first_pass, tiles_sorted, onehot, send_list)
    filtered = (2.0 * second - start.astype(jnp.float32)).astype(jnp.bfloat16)
    total_nodes = length * nrows
    parts, owners = gather_cols(filtered, ncols)
    operated = sorted_apply(filtered, tiles_sorted, onehot, send_list).astype(jnp.bfloat16)
    contract = (((0, 2), (0, 2)), ((), ()))
    portion = jnp.concatenate(parts, axis=1)
    owner_ids = jnp.stack(owners).astype(jnp.int32)
    place = jnp.zeros((ncols,), jnp.int32).at[owner_ids].set(jnp.arange(ncols, dtype=jnp.int32))
    ritz_rows = ritz_matrix.reshape(ncols, columns, ritz_matrix.shape[1])
    weights = jnp.take(ritz_rows, owner_ids, axis=0, mode="clip").reshape(ritz_matrix.shape)
    turned = jnp.einsum("ij,bic->jbc", weights, portion, preferred_element_type=jnp.float32)
    rotated = turned.astype(jnp.bfloat16).reshape(ritz_matrix.shape[1], length)
    lhs = jnp.concatenate([filtered, operated], axis=1)
    both = lax.dot_general(lhs, portion, contract, preferred_element_type=jnp.float32)
    both = both.reshape(2, columns, ncols, columns)
    both = jnp.take(both, place, axis=2, mode="clip").reshape(2, columns, ncols * columns)
    both = tree_sum_rows(both, nrows)
    gram_matrix = both[0] / total_nodes
    projected = both[1] / total_nodes
    return (rotated, gram_matrix, projected)


def solution(mesh):
    return jax.shard_map(
        body,
        mesh=mesh,
        in_specs=(
            P("cols", "rows"),
            P("rows", None, None),
            P("rows", None),
            P("rows", None),
            P("rows", None),
            P(None, "cols"),
        ),
        out_specs=(P("cols", "rows"), P("cols", None), P("cols", None)),
        check_vma=False,
    )
```

```python
import jax
import jax.numpy as jnp
from jax import lax
from jax.sharding import PartitionSpec as P


def plan_slots(tile_row, tile_src, send_list):
    nrows, slot = send_list.shape
    ntiles = tile_src.shape[-1]
    nblocks = ntiles - nrows * slot
    me = lax.axis_index("rows")
    src = tile_src.reshape(-1)
    peer = (src - nblocks) // slot
    shift = (me - peer) % nrows
    moved = nblocks + shift * slot + (src - nblocks) % slot
    slots = jnp.where(src < nblocks, src, moved)
    hit = slots[None, :] == jnp.arange(ntiles, dtype=jnp.int32)[:, None]
    tiles = jnp.arange(ntiles, dtype=jnp.int32)[None, :]
    order = jnp.sum(jnp.where(hit, tiles, 0), axis=1)
    rowof = jnp.sum(jnp.where(hit, tile_row.reshape(1, -1), 0), axis=1)
    return order, rowof, slots


def exchange(blocked, send_list):
    nrows, slot = send_list.shape
    me = lax.axis_index("rows")
    dests = (me + jnp.arange(nrows, dtype=jnp.int32)) % nrows
    wanted = jnp.take(send_list, dests, axis=0, mode="clip").reshape(-1)
    outgoing = jnp.take(blocked, wanted, axis=0, mode="clip")
    pieces = []
    for shift in range(1, nrows):
        chunk = outgoing[shift * slot:(shift + 1) * slot]
        pairs = [(i, (i + shift) % nrows) for i in range(nrows)]
        pieces.append(lax.ppermute(chunk, "rows", pairs))
    return outgoing[:slot], pieces


def row_sum(onehot, products):
    return jnp.einsum("bj,jkr->bkr", onehot, products, precision=lax.Precision.HIGH)


def products_of(sources, tiles):
    return jnp.einsum("jkc,jrc->jkr", sources, tiles, preferred_element_type=jnp.float32)


def first_apply(by_vector, blocked, tile_vals, tile_row, tile_src, send_list):
    nblocks = blocked.shape[0]
    outgoing = jnp.take(by_vector, send_list.reshape(-1), axis=1, mode="clip")
    incoming = lax.all_to_all(outgoing, "rows", 1, 1, tiled=True)
    sources = jnp.concatenate([blocked, incoming.transpose(1, 0, 2)], axis=0)
    chosen = jnp.take(sources, tile_src.reshape(-1), axis=0, mode="clip")
    products = products_of(chosen, tile_vals)
    onehot = (tile_row.reshape(1, -1) == jnp.arange(nblocks, dtype=jnp.int32)[:, None]).astype(jnp.float32)
    return row_sum(onehot, products)


def sorted_apply(blocked, tiles_sorted, onehot, send_list):
    nblocks = blocked.shape[0]
    slot = send_list.shape[1]
    own_self, pieces = exchange(blocked, send_list)
    split = nblocks + slot
    own = products_of(jnp.concatenate([blocked, own_self], axis=0), tiles_sorted[:split])
    out = row_sum(onehot[:, :split], own)
    received = products_of(jnp.concatenate(pieces, axis=0), tiles_sorted[split:])
    return out + row_sum(onehot[:, split:], received)


def tree_sum_rows(value, nrows):
    step = 1
    if nrows % 2 == 0 and nrows <= 8:
        value = value + lax.ppermute(value, "rows", [(i, i ^ 1) for i in range(nrows)])
        groups = nrows // 2
        me = lax.axis_index("rows") // 2
        got = [value]
        for shift in range(1, groups):
            pairs = [(i, (i + 2 * shift) % nrows) for i in range(nrows)]
            got.append(lax.ppermute(value, "rows", pairs))
        owners = (me - jnp.arange(groups, dtype=jnp.int32)) % groups
        place = jnp.zeros((groups,), jnp.int32).at[owners].set(jnp.arange(groups, dtype=jnp.int32))
        ordered = jnp.take(jnp.stack(got), place, axis=0, mode="clip")
        total = ordered[0]
        for n in range(1, groups):
            total = total + ordered[n]
        return total
    while step < nrows:
        pairs = [(i, i ^ step) for i in range(nrows)]
        value = value + lax.ppermute(value, "rows", pairs)
        step *= 2
    return value


def gather_cols(piece, ncols):
    me = lax.axis_index("cols")
    parts, owners = [piece], [me]
    for shift in range(1, ncols):
        pairs = [(i, (i + shift) % ncols) for i in range(ncols)]
        parts.append(lax.ppermute(piece, "cols", pairs))
        owners.append((me - shift) % ncols)
    return parts, owners


def body(vectors, tile_vals, tile_row, tile_src, send_list, ritz_matrix):
    columns, length = vectors.shape
    side = tile_vals.shape[1]
    nblocks = length // side
    nrows = lax.axis_size("rows")
    ncols = lax.axis_size("cols")
    plan = plan_slots(tile_row, tile_src, send_list)
    by_vector = vectors.reshape(columns, nblocks, side)
    start = by_vector.transpose(1, 0, 2)
    first_pass = first_apply(by_vector, start, tile_vals, tile_row, tile_src, send_list).astype(jnp.bfloat16)
    order, rowof, _ = plan
    tiles_sorted = jnp.take(tile_vals, order, axis=0, mode="clip")
    onehot = (rowof[None, :] == jnp.arange(nblocks, dtype=jnp.int32)[:, None]).astype(jnp.float32)
    second = sorted_apply(first_pass, tiles_sorted, onehot, send_list)
    filtered = (2.0 * second - start.astype(jnp.float32)).astype(jnp.bfloat16)
    total_nodes = length * nrows
    parts, owners = gather_cols(filtered, ncols)
    operated = sorted_apply(filtered, tiles_sorted, onehot, send_list).astype(jnp.bfloat16)
    contract = (((0, 2), (0, 2)), ((), ()))
    portion = jnp.concatenate(parts, axis=1)
    owner_ids = jnp.stack(owners).astype(jnp.int32)
    place = jnp.zeros((ncols,), jnp.int32).at[owner_ids].set(jnp.arange(ncols, dtype=jnp.int32))
    ritz_rows = ritz_matrix.reshape(ncols, columns, ritz_matrix.shape[1])
    weights = jnp.take(ritz_rows, owner_ids, axis=0, mode="clip").reshape(ritz_matrix.shape)
    turned = jnp.einsum("ij,bic->jbc", weights, portion, preferred_element_type=jnp.float32)
    rotated = turned.astype(jnp.bfloat16).reshape(ritz_matrix.shape[1], length)
    lhs = jnp.concatenate([filtered, operated], axis=1)
    both = lax.dot_general(lhs, portion, contract, preferred_element_type=jnp.float32)
    both = both.reshape(2, columns, ncols, columns)
    both = jnp.take(both, place, axis=2, mode="clip").reshape(2, columns, ncols * columns)
    both = tree_sum_rows(both, nrows)
    gram_matrix = both[0] / total_nodes
    projected = both[1] / total_nodes
    return (rotated, gram_matrix, projected)


def solution(mesh):
    return jax.shard_map(
        body,
        mesh=mesh,
        in_specs=(
            P("cols", "rows"),
            P("rows", None, None),
            P("rows", None),
            P("rows", None),
            P("rows", None),
            P(None, "cols"),
        ),
        out_specs=(P("cols", "rows"), P("cols", None), P("cols", None)),
        check_vma=False,
    )
```

```python
import jax
import jax.numpy as jnp
from jax import lax
from jax.sharding import PartitionSpec as P


def plan_slots(tile_row, tile_src, send_list):
    nrows, slot = send_list.shape
    ntiles = tile_src.shape[-1]
    nblocks = ntiles - nrows * slot
    me = lax.axis_index("rows")
    src = tile_src.reshape(-1)
    peer = (src - nblocks) // slot
    shift = (me - peer) % nrows
    moved = nblocks + shift * slot + (src - nblocks) % slot
    slots = jnp.where(src < nblocks, src, moved)
    hit = slots[None, :] == jnp.arange(ntiles, dtype=jnp.int32)[:, None]
    tiles = jnp.arange(ntiles, dtype=jnp.int32)[None, :]
    order = jnp.sum(jnp.where(hit, tiles, 0), axis=1)
    rowof = jnp.sum(jnp.where(hit, tile_row.reshape(1, -1), 0), axis=1)
    return order, rowof, slots


def exchange(blocked, send_list):
    nrows, slot = send_list.shape
    me = lax.axis_index("rows")
    dests = (me + jnp.arange(nrows, dtype=jnp.int32)) % nrows
    wanted = jnp.take(send_list, dests, axis=0, mode="clip").reshape(-1)
    outgoing = jnp.take(blocked, wanted, axis=0, mode="clip")
    pieces = []
    for shift in range(1, nrows):
        chunk = outgoing[shift * slot:(shift + 1) * slot]
        pairs = [(i, (i + shift) % nrows) for i in range(nrows)]
        pieces.append(lax.ppermute(chunk, "rows", pairs))
    return outgoing[:slot], pieces


def row_sum(onehot, products):
    return jnp.einsum("bj,jkr->bkr", onehot, products, precision=lax.Precision.HIGH)


def products_of(sources, tiles):
    return jnp.einsum("jkc,jrc->jkr", sources, tiles, preferred_element_type=jnp.float32)


def first_apply(by_vector, blocked, tile_vals, tile_row, tile_src, send_list):
    nblocks = blocked.shape[0]
    outgoing = jnp.take(by_vector, send_list.reshape(-1), axis=1, mode="clip")
    incoming = lax.all_to_all(outgoing, "rows", 1, 1, tiled=True)
    sources = jnp.concatenate([blocked, incoming.transpose(1, 0, 2)], axis=0)
    chosen = jnp.take(sources, tile_src.reshape(-1), axis=0, mode="clip")
    products = products_of(chosen, tile_vals)
    onehot = (tile_row.reshape(1, -1) == jnp.arange(nblocks, dtype=jnp.int32)[:, None]).astype(jnp.float32)
    return row_sum(onehot, products)


def sorted_apply(blocked, tiles_sorted, onehot, send_list):
    nblocks = blocked.shape[0]
    slot = send_list.shape[1]
    own_self, pieces = exchange(blocked, send_list)
    split = nblocks
    own = products_of(blocked, tiles_sorted[:split])
    out = row_sum(onehot[:, :split], own)
    received = products_of(jnp.concatenate([own_self] + pieces, axis=0), tiles_sorted[split:])
    return out + row_sum(onehot[:, split:], received)


def tree_sum_rows(value, nrows):
    step = 1
    if nrows % 2 == 0 and nrows <= 8:
        value = value + lax.ppermute(value, "rows", [(i, i ^ 1) for i in range(nrows)])
        groups = nrows // 2
        me = lax.axis_index("rows") // 2
        got = [value]
        for shift in range(1, groups):
            pairs = [(i, (i + 2 * shift) % nrows) for i in range(nrows)]
            got.append(lax.ppermute(value, "rows", pairs))
        owners = (me - jnp.arange(groups, dtype=jnp.int32)) % groups
        place = jnp.zeros((groups,), jnp.int32).at[owners].set(jnp.arange(groups, dtype=jnp.int32))
        ordered = jnp.take(jnp.stack(got), place, axis=0, mode="clip")
        total = ordered[0]
        for n in range(1, groups):
            total = total + ordered[n]
        return total
    while step < nrows:
        pairs = [(i, i ^ step) for i in range(nrows)]
        value = value + lax.ppermute(value, "rows", pairs)
        step *= 2
    return value


def gather_cols(piece, ncols):
    me = lax.axis_index("cols")
    parts, owners = [piece], [me]
    for shift in range(1, ncols):
        pairs = [(i, (i + shift) % ncols) for i in range(ncols)]
        parts.append(lax.ppermute(piece, "cols", pairs))
        owners.append((me - shift) % ncols)
    return parts, owners


def body(vectors, tile_vals, tile_row, tile_src, send_list, ritz_matrix):
    columns, length = vectors.shape
    side = tile_vals.shape[1]
    nblocks = length // side
    nrows = lax.axis_size("rows")
    ncols = lax.axis_size("cols")
    plan = plan_slots(tile_row, tile_src, send_list)
    by_vector = vectors.reshape(columns, nblocks, side)
    start = by_vector.transpose(1, 0, 2)
    first_pass = first_apply(by_vector, start, tile_vals, tile_row, tile_src, send_list).astype(jnp.bfloat16)
    order, rowof, _ = plan
    tiles_sorted = jnp.take(tile_vals, order, axis=0, mode="clip")
    onehot = (rowof[None, :] == jnp.arange(nblocks, dtype=jnp.int32)[:, None]).astype(jnp.float32)
    second = sorted_apply(first_pass, tiles_sorted, onehot, send_list)
    filtered = (2.0 * second - start.astype(jnp.float32)).astype(jnp.bfloat16)
    total_nodes = length * nrows
    parts, owners = gather_cols(filtered, ncols)
    operated = sorted_apply(filtered, tiles_sorted, onehot, send_list).astype(jnp.bfloat16)
    contract = (((0, 2), (0, 2)), ((), ()))
    portion = jnp.concatenate(parts, axis=1)
    owner_ids = jnp.stack(owners).astype(jnp.int32)
    place = jnp.zeros((ncols,), jnp.int32).at[owner_ids].set(jnp.arange(ncols, dtype=jnp.int32))
    ritz_rows = ritz_matrix.reshape(ncols, columns, ritz_matrix.shape[1])
    weights = jnp.take(ritz_rows, owner_ids, axis=0, mode="clip").reshape(ritz_matrix.shape)
    turned = jnp.einsum("ij,bic->jbc", weights, portion, preferred_element_type=jnp.float32)
    rotated = turned.astype(jnp.bfloat16).reshape(ritz_matrix.shape[1], length)
    lhs = jnp.concatenate([filtered, operated], axis=1)
    both = lax.dot_general(lhs, portion, contract, preferred_element_type=jnp.float32)
    both = both.reshape(2, columns, ncols, columns)
    both = jnp.take(both, place, axis=2, mode="clip").reshape(2, columns, ncols * columns)
    both = tree_sum_rows(both, nrows)
    gram_matrix = both[0] / total_nodes
    projected = both[1] / total_nodes
    return (rotated, gram_matrix, projected)


def solution(mesh):
    return jax.shard_map(
        body,
        mesh=mesh,
        in_specs=(
            P("cols", "rows"),
            P("rows", None, None),
            P("rows", None),
            P("rows", None),
            P("rows", None),
            P(None, "cols"),
        ),
        out_specs=(P("cols", "rows"), P("cols", None), P("cols", None)),
        check_vma=False,
    )
```
